128 devices in a mesh: fsdp: 32 (over y, z, core), seq: 4 (over x).
Axes of the slice: x: 4, y: 4, z: 4, core: 2. Of those that a mesh axis runs over, the one named last changes fastest.
Arguments:
- draft_tokens: bfloat16 [32768, 2048], P('fsdp'), may hold values from -6 to 6
- draft_gate: bfloat16 [2048, 4096], P('fsdp', 'seq'), may hold values from -0.125 to 0.125
- draft_up: bfloat16 [2048, 4096], P('fsdp', 'seq'), may hold values from -0.125 to 0.125
- draft_head: float32 [4096], P('seq'), may hold values from -0.75 to 0.75
- verifier_rows: bfloat16 [32768, 8192], P(('fsdp', 'seq')), may hold values from -6 to 6
- norm_gain: float32 [8192], replicated, may hold values from 0.5 to 1.5
- key_weight: bfloat16 [8192, 512], P('fsdp'), may hold values from -0.06629126 to 0.06629126
- value_weight: bfloat16 [8192, 512], P('fsdp'), may hold values from -0.0625 to 0.0625
- pool_query: float32 [4, 4, 128], replicated, may hold values from -32 to 32
- flags: int32 [1024], P(('fsdp', 'seq')), may hold values from 0 to 1, as said below
- owner: int32 [1024], P(('fsdp', 'seq')), may hold values from 0 to 3
Outputs:
- draft_score: float32 [1024], P(('fsdp', 'seq'))
- verdict: bfloat16 [1024, 512], P(('fsdp', 'seq'))
The draws below stay inside these ranges and needn't reach their ends.
Inputs may be any that keep to these rules, and one draw needn't show every extreme that they name: `flags`: on the 8 segments of one device, at most 4 flagged segments share an owner lane, and on every device exactly 4 flagged segments share one lane.
All inputs are finite; a program needn't handle non-finite values.
Results may differ from the reference program's by a relative error of at most 0.009.
Values may be sent and summed in bfloat16 or wider, within the bound.
No kernel may reach another device: no remote copies, remote signals or barrier semaphores. Data moves between devices by JAX's collectives and lax.ppermute only.
A program may use at most 128 MiB of HBM per device.

```python
import math
import jax
import jax.numpy as jnp
from jax import lax

DD = 2048
DFF = 4096
DV = 8192
KVH = 4
HD = 128
CATS = 4
SEGL = 32
SEG_DEV = 8
CAP = 4
REQ_SEGS = 32
SEGS = 1024
N_FSDP = 32


def routing_pair(key):
    blocks = SEGS // SEG_DEV
    key_base = jax.random.fold_in(key, 11)
    key_extra = jax.random.fold_in(key, 12)
    key_shift = jax.random.fold_in(key, 13)
    key_first = jax.random.fold_in(key, 14)
    key_want = jax.random.fold_in(key, 15)
    base = jax.random.randint(key_base, (blocks, SEG_DEV), 0, CATS)
    extra = jax.random.randint(key_extra, (blocks, SEG_DEV), 0, CATS)
    shift = jax.random.randint(key_shift, (blocks, 1), 0, CATS)
    lanes = (jnp.minimum(base, extra) + shift) % CATS
    first_lane = jax.random.randint(key_first, (blocks, 1), 0, CATS)
    position = jnp.arange(SEG_DEV, dtype=jnp.int32)
    forced = position[None, :] < CAP
    lanes = jnp.where(forced, first_lane, lanes)
    wanted = (jax.random.randint(key_want, (blocks, SEG_DEV), 0, 4) > 0) | forced
    earlier = (lanes[:, :, None] == lanes[:, None, :]) & wanted[:, None, :] & (position[None, None, :] < position[None, :, None])
    ranking = jnp.sum(earlier.astype(jnp.int32), axis=2)
    chosen = (wanted & (ranking < CAP)).astype(jnp.int32)
    return (chosen.reshape(SEGS), lanes.astype(jnp.int32).reshape(SEGS))


def draw_flags(key, part):
    return routing_pair(key)[0]


def draw_owner(key, part):
    return routing_pair(key)[1]


def draw_verifier_rows(key, part):
    rows_total = SEGS * SEGL
    key_rows = jax.random.fold_in(key, 31)
    rows = jnp.clip(jax.random.normal(key_rows, (rows_total, DV), jnp.float32), -6.0, 6.0)
    return rows.astype(jnp.bfloat16)


def draw_key_weight(key, part):
    key_main = jax.random.fold_in(key, 41)
    bound = 6.0 * DV ** (-0.5)
    weights = jnp.clip(jax.random.normal(key_main, (DV, KVH * HD), jnp.float32) * DV ** (-0.5), -bound, bound)
    return weights.astype(jnp.bfloat16)


def draw_pool_query(key, part):
    key_main = jax.random.fold_in(key, 51)
    query = jnp.clip(jax.random.normal(key_main, (CATS, KVH, HD), jnp.float32), -6.0, 6.0)
    return query


def steps_of(key, dims, pieces, least, top_value):
    def one(dim, blocks):
        draws = jax.random.uniform(jax.random.fold_in(jax.random.fold_in(key, 6), dim), (blocks,), jnp.float32, least / len(pieces), top_value / len(pieces))
        return jnp.repeat(jnp.exp(draws), dims[dim] // blocks).reshape((-1,) + (1,) * (len(dims) - dim - 1))

    factor_of = one(*pieces[0])
    for cut in pieces[1:]:
        factor_of = factor_of * one(*cut)
    return factor_of


def centred(stream_key, shape, spread, most, cuts=(), held_as=jnp.bfloat16):
    gain = steps_of(stream_key, shape, cuts, -0.22, 0.18) if cuts else 1.0
    array = jax.random.normal(stream_key, shape, jnp.float32) * spread * gain
    return jnp.minimum(jnp.maximum(array, -most), most).astype(held_as)


def setup_inputs(seed: int = 0) -> dict:
    seeds = jax.random.split(jax.random.key(seed), 12)
    draft_tokens = centred(seeds[0], (SEGS * SEGL, DD), 1.0, 6.0, ((0, 32),))
    draft_gate = centred(seeds[1], (DD, DFF), DD ** -0.5, 0.125, ((0, 32), (1, 4)))
    draft_up = centred(seeds[2], (DD, DFF), DD ** -0.5, 0.125, ((0, 32), (1, 4)))
    draft_head = centred(seeds[3], (DFF,), (DFF // 64) ** -0.5, 0.75, ((0, 4),), jnp.float32)
    verifier_rows = draw_verifier_rows(jax.random.fold_in(seeds[11], 71), 0)
    norm_gain = jnp.clip(1.0 + 0.1 * jax.random.normal(seeds[5], (DV,), jnp.float32), 0.5, 1.5)
    key_weight = draw_key_weight(jax.random.fold_in(seeds[11], 71), 0)
    value_weight = centred(seeds[7], (DV, KVH * HD), DV ** -0.5, 0.0625, ((0, 32),))
    pool_query = draw_pool_query(jax.random.fold_in(seeds[11], 71), 0)
    flags = draw_flags(jax.random.fold_in(seeds[11], 71), 0)
    owner = draw_owner(jax.random.fold_in(seeds[11], 71), 0)
    return dict(draft_tokens=draft_tokens, draft_gate=draft_gate, draft_up=draft_up, draft_head=draft_head, verifier_rows=verifier_rows, norm_gain=norm_gain, key_weight=key_weight, value_weight=value_weight, pool_query=pool_query, flags=flags, owner=owner)


eps = 1e-05

def normalize_rows(rows, norm_gain):
    values = rows.astype(jnp.float32)
    scale = lax.rsqrt(lax.optimization_barrier(jnp.mean(values * values, axis=-1, keepdims=True)) + eps)
    return (values * scale * norm_gain).astype(jnp.bfloat16)

def segment_pool(seg_keys, seg_values, queries, head_size):
    scores = jnp.einsum('sthd,shd->sth', seg_keys, queries, precision=lax.Precision.HIGHEST) / math.sqrt(head_size)
    scores = scores - lax.optimization_barrier(jnp.max(scores, axis=1, keepdims=True))
    weights = jnp.exp(scores)
    weights = weights / lax.optimization_barrier(jnp.sum(weights, axis=1, keepdims=True))
    summary_key = jnp.einsum('sth,sthd->shd', weights, seg_keys, precision=lax.Precision.HIGHEST)
    summary_value = jnp.einsum('sth,sthd->shd', weights, seg_values, precision=lax.Precision.HIGHEST)
    return (summary_key, summary_value)

def cross_pool(query_keys, key_all, value_all, live_all, head_size):
    scores = jnp.einsum('jhd,ihd->jhi', query_keys, key_all, precision=lax.Precision.HIGHEST) / math.sqrt(head_size)
    scores = jnp.where(live_all[None, None, :], scores, -1e+30)
    highest = lax.optimization_barrier(jnp.max(scores, axis=2, keepdims=True))
    weights = jnp.where(live_all[None, None, :], jnp.exp(scores - highest), 0.0)
    total = lax.optimization_barrier(jnp.sum(weights, axis=2, keepdims=True))
    return jnp.einsum('jhi,ihd->jhd', weights, value_all, precision=lax.Precision.HIGHEST) / total

def reference(draft_tokens, draft_gate, draft_up, draft_head, verifier_rows, norm_gain, key_weight, value_weight, pool_query, flags, owner):
    blocks = draft_tokens.reshape(N_FSDP, REQ_SEGS * SEGL, DD)

    def draft_block(rows):
        gate = jnp.dot(rows, draft_gate, preferred_element_type=jnp.float32)
        upward = jnp.dot(rows, draft_up, preferred_element_type=jnp.float32)
        return lax.optimization_barrier(jnp.sum(jax.nn.silu(gate) * upward * draft_head, axis=1))
    token_score = lax.map(draft_block, blocks).reshape(SEGS, SEGL)
    draft_score = lax.optimization_barrier(jnp.mean(token_score, axis=1))

    def verify_request(item):
        rows, live_flags, lanes = item
        normed = normalize_rows(rows, norm_gain)
        seg_keys = jnp.dot(normed, key_weight, preferred_element_type=jnp.float32).reshape(REQ_SEGS, SEGL, KVH, HD)
        seg_values = jnp.dot(normed, value_weight, preferred_element_type=jnp.float32).reshape(REQ_SEGS, SEGL, KVH, HD)
        queries = pool_query[lanes]
        summary_key, summary_value = segment_pool(seg_keys, seg_values, queries, HD)
        pooled = cross_pool(summary_key, summary_key, summary_value, live_flags == 1, HD)
        return pooled.reshape(REQ_SEGS, KVH * HD)
    pooled = lax.map(verify_request, (verifier_rows.reshape(N_FSDP, REQ_SEGS * SEGL, DV), flags.reshape(N_FSDP, REQ_SEGS), owner.reshape(N_FSDP, REQ_SEGS)))
    pooled = pooled.reshape(SEGS, KVH * HD)
    verdict = jnp.where(flags[:, None] == 1, jax.nn.sigmoid(draft_score)[:, None] * pooled, 0.0).astype(jnp.bfloat16)
    return (draft_score, verdict)
```

```python
import math

import jax
import jax.numpy as jnp
from jax import lax
from jax.sharding import PartitionSpec as P

KVH = 4
HD = 128
SEGL = 32


eps = 1e-05


def normalize_rows(rows, norm_gain):
    values = rows.astype(jnp.float32)
    scale = lax.rsqrt(jnp.mean(values * values, axis=-1, keepdims=True) + eps)
    return (values * scale * norm_gain).astype(jnp.bfloat16)


def segment_pool(seg_keys, seg_values, queries, head_size):
    scores = jnp.einsum(
        "sthd,shd->sth", seg_keys, queries, precision=lax.Precision.HIGHEST
    ) / math.sqrt(head_size)
    scores = scores - jnp.max(scores, axis=1, keepdims=True)
    weights = jnp.exp(scores)
    weights = weights / jnp.sum(weights, axis=1, keepdims=True)
    summary_key = jnp.einsum("sth,sthd->shd", weights, seg_keys, precision=lax.Precision.HIGHEST)
    summary_value = jnp.einsum(
        "sth,sthd->shd", weights, seg_values, precision=lax.Precision.HIGHEST
    )
    return (summary_key, summary_value)


def cross_pool(query_keys, key_all, value_all, live_all, head_size):
    scores = jnp.einsum(
        "jhd,ihd->jhi", query_keys, key_all, precision=lax.Precision.HIGHEST
    ) / math.sqrt(head_size)
    scores = jnp.where(live_all[None, None, :], scores, -1e30)
    highest = jnp.max(scores, axis=2, keepdims=True)
    weights = jnp.where(live_all[None, None, :], jnp.exp(scores - highest), 0.0)
    total = jnp.sum(weights, axis=2, keepdims=True)
    return jnp.einsum("jhi,ihd->jhd", weights, value_all, precision=lax.Precision.HIGHEST) / total


def local(
    draft_tokens,
    draft_gate,
    draft_up,
    draft_head,
    verifier_rows,
    norm_gain,
    key_weight,
    value_weight,
    pool_query,
    flags,
    owner,
):
    seg_count = flags.shape[0]
    n_seq = lax.axis_size("seq")
    n_fsdp = lax.axis_size("fsdp")
    d_rows, d_cols = draft_gate.shape
    v_rows = key_weight.shape[0]
    kv_cols = key_weight.shape[1]
    kv_block = jnp.concatenate([key_weight, value_weight], axis=1)
    kv_block = kv_block.reshape(-1, d_cols)
    block = jnp.concatenate([draft_gate, draft_up, kv_block], axis=0)
    gathered = lax.all_gather(block, "fsdp", axis=0, tiled=False)
    gate_w = gathered[:, :d_rows].reshape(n_fsdp * d_rows, d_cols)
    up_w = gathered[:, d_rows : 2 * d_rows].reshape(n_fsdp * d_rows, d_cols)
    kv_w = gathered[:, 2 * d_rows :].reshape(n_fsdp * v_rows, 2 * kv_cols)

    gate = jnp.dot(draft_tokens, gate_w, preferred_element_type=jnp.float32)
    upward = jnp.dot(draft_tokens, up_w, preferred_element_type=jnp.float32)
    partial_scores = jnp.sum(jax.nn.silu(gate) * upward * draft_head[None, :], axis=1)

    normed = normalize_rows(verifier_rows, norm_gain)
    seg_kv = jnp.dot(normed, kv_w, preferred_element_type=jnp.float32)
    seg_keys = seg_kv[:, :kv_cols]
    seg_values = seg_kv[:, kv_cols:]
    lane_pick = (
        owner[:, None] == jnp.arange(pool_query.shape[0], dtype=jnp.int32)[None, :]
    ).astype(jnp.float32)
    queries = jnp.einsum("sc,chd->shd", lane_pick, pool_query, precision=lax.Precision.HIGHEST)
    summary_key, summary_value = segment_pool(
        seg_keys.reshape(seg_count, SEGL, KVH, HD),
        seg_values.reshape(seg_count, SEGL, KVH, HD),
        queries,
        HD,
    )
    width = KVH * HD
    live_row = jnp.zeros((1, width), jnp.float32).at[0, :seg_count].set(flags.astype(jnp.float32))
    tail = jnp.concatenate(
        [
            partial_scores.reshape(-1, width),
            summary_key.reshape(seg_count, width),
            summary_value.reshape(seg_count, width),
            live_row,
        ],
        axis=0,
    )
    tail_all = lax.all_gather(tail, "seq", axis=0, tiled=False)
    score_rows = partial_scores.shape[0] // width
    scores_all = tail_all[:, :score_rows].reshape(n_seq, -1)
    own = lax.axis_index("seq")
    own_tokens = seg_count * SEGL
    token_scores = jnp.sum(
        lax.dynamic_slice_in_dim(scores_all, own * own_tokens, own_tokens, axis=1), axis=0
    )
    draft_score = jnp.mean(token_scores.reshape(seg_count, SEGL), axis=1)
    key_all = tail_all[:, score_rows : score_rows + seg_count].reshape(-1, KVH, HD)
    value_all = tail_all[:, score_rows + seg_count : score_rows + 2 * seg_count].reshape(-1, KVH, HD)
    live_all = tail_all[:, score_rows + 2 * seg_count, :seg_count].reshape(-1)
    pooled = cross_pool(
        summary_key,
        key_all,
        value_all,
        live_all > 0.5,
        HD,
    )
    own_pooled = pooled.reshape(seg_count, KVH * HD)
    verdict = jnp.where(
        flags[:, None] == 1, jax.nn.sigmoid(draft_score)[:, None] * own_pooled, 0.0
    ).astype(jnp.bfloat16)
    return (draft_score, verdict)


def solution(mesh):
    return jax.shard_map(
        local,
        mesh=mesh,
        in_specs=(
            P("fsdp", None),
            P("fsdp", "seq"),
            P("fsdp", "seq"),
            P("seq"),
            P(("fsdp", "seq"), None),
            P(),
            P("fsdp", None),
            P("fsdp", None),
            P(),
            P(("fsdp", "seq")),
            P(("fsdp", "seq")),
        ),
        out_specs=(P(("fsdp", "seq")), P(("fsdp", "seq"), None)),
        check_vma=False,
    )
```

```python
import math

import jax
import jax.numpy as jnp
from jax import lax
from jax.experimental import pallas as pl
from jax.experimental.pallas import tpu as pltpu
from jax.sharding import PartitionSpec as P

KVH = 4
HD = 128
SEGL = 32


eps = 1e-05


def normalize_rows(rows, norm_gain):
    values = rows.astype(jnp.float32)
    scale = lax.rsqrt(jnp.mean(values * values, axis=-1, keepdims=True) + eps)
    return (values * scale * norm_gain).astype(jnp.bfloat16)


def segment_pool(seg_keys, seg_values, queries, head_size):
    scores = jnp.einsum(
        "sthd,shd->sth", seg_keys, queries, precision=lax.Precision.HIGHEST
    ) / math.sqrt(head_size)
    scores = scores - jnp.max(scores, axis=1, keepdims=True)
    weights = jnp.exp(scores)
    weights = weights / jnp.sum(weights, axis=1, keepdims=True)
    summary_key = jnp.einsum("sth,sthd->shd", weights, seg_keys, precision=lax.Precision.HIGHEST)
    summary_value = jnp.einsum(
        "sth,sthd->shd", weights, seg_values, precision=lax.Precision.HIGHEST
    )
    return (summary_key, summary_value)


def cross_pool(query_keys, key_all, value_all, live_all, head_size):
    scores = jnp.einsum(
        "jhd,ihd->jhi", query_keys, key_all, precision=lax.Precision.HIGHEST
    ) / math.sqrt(head_size)
    scores = jnp.where(live_all[None, None, :], scores, -1e30)
    highest = jnp.max(scores, axis=2, keepdims=True)
    weights = jnp.where(live_all[None, None, :], jnp.exp(scores - highest), 0.0)
    total = jnp.sum(weights, axis=2, keepdims=True)
    return jnp.einsum("jhi,ihd->jhd", weights, value_all, precision=lax.Precision.HIGHEST) / total


def draft_kernel(tok_ref, g_ref, u_ref, head_ref, out_ref, gacc, uacc):
    j = pl.program_id(0)

    @pl.when(j == 0)
    def _():
        gacc[...] = jnp.zeros_like(gacc)
        uacc[...] = jnp.zeros_like(uacc)

    t = tok_ref[...]
    k = g_ref.shape[0] * g_ref.shape[1]
    gacc[...] += jnp.dot(t, g_ref[...].reshape(k, -1), preferred_element_type=jnp.float32)
    uacc[...] += jnp.dot(t, u_ref[...].reshape(k, -1), preferred_element_type=jnp.float32)

    @pl.when(j == pl.num_programs(0) - 1)
    def _():
        g = gacc[...]
        act = g / (1.0 + jnp.exp(-g))
        out_ref[...] = jnp.sum(act * uacc[...] * head_ref[...], axis=1, keepdims=True)


def draft_scores(tokens, gathered, head, row0, d_rows, group):
    n_dev, _, cols = gathered.shape
    n_tok = tokens.shape[0]
    k = group * d_rows
    gate_blk = row0 // d_rows
    return pl.pallas_call(
        draft_kernel,
        grid=(n_dev // group,),
        in_specs=[
            pl.BlockSpec((n_tok, k), lambda j: (0, j)),
            pl.BlockSpec((group, d_rows, cols), lambda j: (j, gate_blk, 0)),
            pl.BlockSpec((group, d_rows, cols), lambda j: (j, gate_blk + 1, 0)),
            pl.BlockSpec((1, cols), lambda j: (0, 0)),
        ],
        out_specs=pl.BlockSpec((n_tok, 1), lambda j: (0, 0)),
        out_shape=jax.ShapeDtypeStruct((n_tok, 1), jnp.float32),
        scratch_shapes=[
            pltpu.VMEM((n_tok, cols), jnp.float32),
            pltpu.VMEM((n_tok, cols), jnp.float32),
        ],
    )(tokens, gathered, gathered, head.reshape(1, cols))[:, 0]


def kv_kernel(x_ref, w_ref, out_ref):
    j = pl.program_id(0)

    @pl.when(j == 0)
    def _():
        out_ref[...] = jnp.zeros_like(out_ref)

    k = w_ref.shape[0] * w_ref.shape[1]
    out_ref[...] += jnp.dot(x_ref[...], w_ref[...].reshape(k, -1), preferred_element_type=jnp.float32)


def kv_project(normed, gathered, v_rows, group):
    n_dev, _, cols = gathered.shape
    n_tok = normed.shape[0]
    k = group * v_rows
    return pl.pallas_call(
        kv_kernel,
        grid=(n_dev // group,),
        in_specs=[
            pl.BlockSpec((n_tok, k), lambda j: (0, j)),
            pl.BlockSpec((group, v_rows, cols), lambda j: (j, 0, 0)),
        ],
        out_specs=pl.BlockSpec((n_tok, cols), lambda j: (0, 0)),
        out_shape=jax.ShapeDtypeStruct((n_tok, cols), jnp.float32),
    )(normed, gathered)


def local(
    draft_tokens,
    draft_gate,
    draft_up,
    draft_head,
    verifier_rows,
    norm_gain,
    key_weight,
    value_weight,
    pool_query,
    flags,
    owner,
):
    seg_count = flags.shape[0]
    n_seq = lax.axis_size("seq")
    n_fsdp = lax.axis_size("fsdp")
    d_rows, d_cols = draft_gate.shape
    v_rows = key_weight.shape[0]
    kv_cols = key_weight.shape[1]
    kv_block = jnp.concatenate([key_weight, value_weight], axis=1)
    kv_block = kv_block.reshape(-1, d_cols)
    block = jnp.concatenate([kv_block, draft_gate, draft_up], axis=0)
    gathered = lax.all_gather(block, "fsdp", axis=0, tiled=False)
    kv_rows = kv_block.shape[0]

    partial_scores = draft_scores(draft_tokens, gathered, draft_head, kv_rows, d_rows, 4)

    normed = normalize_rows(verifier_rows, norm_gain)
    seg_kv = kv_project(normed, gathered, kv_rows, 2)
    seg_keys = seg_kv[:, :kv_cols]
    seg_values = seg_kv[:, kv_cols:]
    lane_pick = (
        owner[:, None] == jnp.arange(pool_query.shape[0], dtype=jnp.int32)[None, :]
    ).astype(jnp.float32)
    queries = jnp.einsum("sc,chd->shd", lane_pick, pool_query, precision=lax.Precision.HIGHEST)
    summary_key, summary_value = segment_pool(
        seg_keys.reshape(seg_count, SEGL, KVH, HD),
        seg_values.reshape(seg_count, SEGL, KVH, HD),
        queries,
        HD,
    )
    width = KVH * HD
    live_row = jnp.zeros((1, width), jnp.float32).at[0, :seg_count].set(flags.astype(jnp.float32))
    tail = jnp.concatenate(
        [
            partial_scores.reshape(-1, width),
            summary_key.reshape(seg_count, width),
            summary_value.reshape(seg_count, width),
            live_row,
        ],
        axis=0,
    )
    tail_all = lax.all_gather(tail, "seq", axis=0, tiled=False)
    score_rows = partial_scores.shape[0] // width
    scores_all = tail_all[:, :score_rows].reshape(n_seq, -1)
    own = lax.axis_index("seq")
    own_tokens = seg_count * SEGL
    token_scores = jnp.sum(
        lax.dynamic_slice_in_dim(scores_all, own * own_tokens, own_tokens, axis=1), axis=0
    )
    draft_score = jnp.mean(token_scores.reshape(seg_count, SEGL), axis=1)
    key_all = tail_all[:, score_rows : score_rows + seg_count].reshape(-1, KVH, HD)
    value_all = tail_all[:, score_rows + seg_count : score_rows + 2 * seg_count].reshape(-1, KVH, HD)
    live_all = tail_all[:, score_rows + 2 * seg_count, :seg_count].reshape(-1)
    pooled = cross_pool(
        summary_key,
        key_all,
        value_all,
        live_all > 0.5,
        HD,
    )
    own_pooled = pooled.reshape(seg_count, KVH * HD)
    verdict = jnp.where(
        flags[:, None] == 1, jax.nn.sigmoid(draft_score)[:, None] * own_pooled, 0.0
    ).astype(jnp.bfloat16)
    return (draft_score, verdict)


def solution(mesh):
    return jax.shard_map(
        local,
        mesh=mesh,
        in_specs=(
            P("fsdp", None),
            P("fsdp", "seq"),
            P("fsdp", "seq"),
            P("seq"),
            P(("fsdp", "seq"), None),
            P(),
            P("fsdp", None),
            P("fsdp", None),
            P(),
            P(("fsdp", "seq")),
            P(("fsdp", "seq")),
        ),
        out_specs=(P(("fsdp", "seq")), P(("fsdp", "seq"), None)),
        check_vma=False,
    )
```

```python
import math

import jax
import jax.numpy as jnp
from jax import lax
from jax.experimental import pallas as pl
from jax.experimental.pallas import tpu as pltpu
from jax.sharding import PartitionSpec as P

KVH = 4
HD = 128
SEGL = 32


eps = 1e-05


def normalize_rows(rows, norm_gain):
    values = rows.astype(jnp.float32)
    scale = lax.rsqrt(jnp.mean(values * values, axis=-1, keepdims=True) + eps)
    return (values * scale * norm_gain).astype(jnp.bfloat16)


def segment_pool(seg_keys, seg_values, queries, head_size):
    scores = jnp.einsum(
        "sthd,shd->sth", seg_keys, queries, precision=lax.Precision.HIGHEST
    ) / math.sqrt(head_size)
    scores = scores - jnp.max(scores, axis=1, keepdims=True)
    weights = jnp.exp(scores)
    weights = weights / jnp.sum(weights, axis=1, keepdims=True)
    summary_key = jnp.einsum("sth,sthd->shd", weights, seg_keys, precision=lax.Precision.HIGHEST)
    summary_value = jnp.einsum(
        "sth,sthd->shd", weights, seg_values, precision=lax.Precision.HIGHEST
    )
    return (summary_key, summary_value)


def cross_pool(query_keys, key_all, value_all, live_all, head_size):
    scores = jnp.einsum(
        "jhd,ihd->jhi", query_keys, key_all, precision=lax.Precision.HIGHEST
    ) / math.sqrt(head_size)
    scores = jnp.where(live_all[None, None, :], scores, -1e30)
    highest = jnp.max(scores, axis=2, keepdims=True)
    weights = jnp.where(live_all[None, None, :], jnp.exp(scores - highest), 0.0)
    total = jnp.sum(weights, axis=2, keepdims=True)
    return jnp.einsum("jhi,ihd->jhd", weights, value_all, precision=lax.Precision.HIGHEST) / total


def draft_kernel(tok_ref, g_ref, u_ref, head_ref, out_ref, gacc, uacc):
    j = pl.program_id(0)

    @pl.when(j == 0)
    def _():
        gacc[...] = jnp.zeros_like(gacc)
        uacc[...] = jnp.zeros_like(uacc)

    t = tok_ref[...]
    k = g_ref.shape[0] * g_ref.shape[1]
    gacc[...] += jnp.dot(t, g_ref[...].reshape(k, -1), preferred_element_type=jnp.float32)
    uacc[...] += jnp.dot(t, u_ref[...].reshape(k, -1), preferred_element_type=jnp.float32)

    @pl.when(j == pl.num_programs(0) - 1)
    def _():
        g = gacc[...]
        act = g / (1.0 + jnp.exp(-g))
        out_ref[...] = jnp.sum(act * uacc[...] * head_ref[...], axis=1, keepdims=True)


def draft_scores(tokens, gathered, head, row0, d_rows, group):
    n_dev, _, cols = gathered.shape
    n_tok = tokens.shape[0]
    k = group * d_rows
    gate_blk = row0 // d_rows
    return pl.pallas_call(
        draft_kernel,
        grid=(n_dev // group,),
        in_specs=[
            pl.BlockSpec((n_tok, k), lambda j: (0, j)),
            pl.BlockSpec((group, d_rows, cols), lambda j: (j, gate_blk, 0)),
            pl.BlockSpec((group, d_rows, cols), lambda j: (j, gate_blk + 1, 0)),
            pl.BlockSpec((1, cols), lambda j: (0, 0)),
        ],
        out_specs=pl.BlockSpec((n_tok, 1), lambda j: (0, 0)),
        out_shape=jax.ShapeDtypeStruct((n_tok, 1), jnp.float32),
        scratch_shapes=[
            pltpu.VMEM((n_tok, cols), jnp.float32),
            pltpu.VMEM((n_tok, cols), jnp.float32),
        ],
    )(tokens, gathered, gathered, head.reshape(1, cols))[:, 0]


def kv_kernel(x_ref, w_ref, out_ref):
    j = pl.program_id(0)

    @pl.when(j == 0)
    def _():
        out_ref[...] = jnp.zeros_like(out_ref)

    group, rows, _ = w_ref.shape
    acc = jnp.dot(x_ref[:, 0:rows], w_ref[0], preferred_element_type=jnp.float32)
    for i in range(1, group):
        acc += jnp.dot(
            x_ref[:, i * rows : (i + 1) * rows], w_ref[i], preferred_element_type=jnp.float32
        )
    out_ref[...] += acc


def kv_project(normed, gathered, v_rows, group):
    n_dev, _, cols = gathered.shape
    n_tok = normed.shape[0]
    k = group * v_rows
    return pl.pallas_call(
        kv_kernel,
        grid=(n_dev // group,),
        in_specs=[
            pl.BlockSpec((n_tok, k), lambda j: (0, j)),
            pl.BlockSpec((group, v_rows, cols), lambda j: (j, 0, 0)),
        ],
        out_specs=pl.BlockSpec((n_tok, cols), lambda j: (0, 0)),
        out_shape=jax.ShapeDtypeStruct((n_tok, cols), jnp.float32),
    )(normed, gathered)


def local(
    draft_tokens,
    draft_gate,
    draft_up,
    draft_head,
    verifier_rows,
    norm_gain,
    key_weight,
    value_weight,
    pool_query,
    flags,
    owner,
):
    seg_count = flags.shape[0]
    n_seq = lax.axis_size("seq")
    n_fsdp = lax.axis_size("fsdp")
    d_rows, d_cols = draft_gate.shape
    v_rows = key_weight.shape[0]
    kv_cols = key_weight.shape[1]
    kv_block = jnp.concatenate([key_weight, value_weight], axis=1)
    kv_block = kv_block.reshape(-1, d_cols)
    block = jnp.concatenate([kv_block, draft_gate, draft_up], axis=0)
    gathered = lax.all_gather(block, "fsdp", axis=0, tiled=False)
    kv_rows = kv_block.shape[0]


    normed = normalize_rows(verifier_rows, norm_gain)
    seg_kv = kv_project(normed, gathered, kv_rows, 8)
    seg_keys = seg_kv[:, :kv_cols]
    seg_values = seg_kv[:, kv_cols:]
    lane_pick = (
        owner[:, None] == jnp.arange(pool_query.shape[0], dtype=jnp.int32)[None, :]
    ).astype(jnp.float32)
    queries = jnp.einsum("sc,chd->shd", lane_pick, pool_query, precision=lax.Precision.HIGHEST)
    summary_key, summary_value = segment_pool(
        seg_keys.reshape(seg_count, SEGL, KVH, HD),
        seg_values.reshape(seg_count, SEGL, KVH, HD),
        queries,
        HD,
    )
    width = KVH * HD
    live_row = jnp.zeros((1, width), jnp.float32).at[0, :seg_count].set(flags.astype(jnp.float32))
    summary = jnp.concatenate(
        [summary_key.reshape(seg_count, width), summary_value.reshape(seg_count, width), live_row],
        axis=0,
    )
    shifts = range(1, n_seq)
    summary_all = jnp.stack(
        [summary]
        + [lax.ppermute(summary, "seq", [(i, (i + k) % n_seq) for i in range(n_seq)]) for k in shifts]
    )

    partial_scores = draft_scores(draft_tokens, gathered, draft_head, kv_rows, d_rows, 8)
    scores_all = jnp.stack(
        [partial_scores]
        + [
            lax.ppermute(partial_scores, "seq", [(i, (i + k) % n_seq) for i in range(n_seq)])
            for k in shifts
        ]
    )
    own = lax.axis_index("seq")
    own_tokens = seg_count * SEGL
    token_scores = jnp.sum(
        lax.dynamic_slice_in_dim(scores_all, own * own_tokens, own_tokens, axis=1), axis=0
    )
    draft_score = jnp.mean(token_scores.reshape(seg_count, SEGL), axis=1)
    key_all = summary_all[:, :seg_count].reshape(-1, KVH, HD)
    value_all = summary_all[:, seg_count : 2 * seg_count].reshape(-1, KVH, HD)
    live_all = summary_all[:, 2 * seg_count, :seg_count].reshape(-1)
    pooled = cross_pool(
        summary_key,
        key_all,
        value_all,
        live_all > 0.5,
        HD,
    )
    own_pooled = pooled.reshape(seg_count, KVH * HD)
    verdict = jnp.where(
        flags[:, None] == 1, jax.nn.sigmoid(draft_score)[:, None] * own_pooled, 0.0
    ).astype(jnp.bfloat16)
    return (draft_score, verdict)


def solution(mesh):
    return jax.shard_map(
        local,
        mesh=mesh,
        in_specs=(
            P("fsdp", None),
            P("fsdp", "seq"),
            P("fsdp", "seq"),
            P("seq"),
            P(("fsdp", "seq"), None),
            P(),
            P("fsdp", None),
            P("fsdp", None),
            P(),
            P(("fsdp", "seq")),
            P(("fsdp", "seq")),
        ),
        out_specs=(P(("fsdp", "seq")), P(("fsdp", "seq"), None)),
        check_vma=False,
    )
```

```python
import math

import jax
import jax.numpy as jnp
from jax import lax
from jax.experimental import pallas as pl
from jax.experimental.pallas import tpu as pltpu
from jax.sharding import PartitionSpec as P

KVH = 4
HD = 128
SEGL = 32


eps = 1e-05


def normalize_rows(rows, norm_gain):
    values = rows.astype(jnp.float32)
    scale = lax.rsqrt(jnp.mean(values * values, axis=-1, keepdims=True) + eps)
    return (values * scale * norm_gain).astype(jnp.bfloat16)


def segment_pool(seg_keys, seg_values, queries, head_size):
    scores = jnp.sum(seg_keys * queries[:, None], axis=-1) / math.sqrt(head_size)
    scores = scores - jnp.max(scores, axis=1, keepdims=True)
    weights = jnp.exp(scores)
    weights = weights / jnp.sum(weights, axis=1, keepdims=True)
    summary_key = jnp.sum(weights[..., None] * seg_keys, axis=1)
    summary_value = jnp.sum(weights[..., None] * seg_values, axis=1)
    return (summary_key, summary_value)


def cross_pool(query_keys, key_all, value_all, live_all, head_size):
    scores = jnp.sum(query_keys[:, :, None, :] * jnp.swapaxes(key_all, 0, 1)[None], axis=-1)
    scores = scores / math.sqrt(head_size)
    scores = jnp.where(live_all[None, None, :], scores, -1e30)
    highest = jnp.max(scores, axis=2, keepdims=True)
    weights = jnp.where(live_all[None, None, :], jnp.exp(scores - highest), 0.0)
    total = jnp.sum(weights, axis=2, keepdims=True)
    pooled = jnp.sum(weights[..., None] * jnp.swapaxes(value_all, 0, 1)[None], axis=2)
    return pooled / total


def draft_kernel(tok_ref, g_ref, u_ref, head_ref, out_ref, gacc, uacc):
    j = pl.program_id(0)

    @pl.when(j == 0)
    def _():
        gacc[...] = jnp.zeros_like(gacc)
        uacc[...] = jnp.zeros_like(uacc)

    t = tok_ref[...]
    k = g_ref.shape[0] * g_ref.shape[1]
    gacc[...] += jnp.dot(t, g_ref[...].reshape(k, -1), preferred_element_type=jnp.float32)
    uacc[...] += jnp.dot(t, u_ref[...].reshape(k, -1), preferred_element_type=jnp.float32)

    @pl.when(j == pl.num_programs(0) - 1)
    def _():
        g = gacc[...]
        act = g / (1.0 + jnp.exp(-g))
        out_ref[...] = jnp.sum(act * uacc[...] * head_ref[...], axis=1, keepdims=True)


def draft_scores(tokens, gathered, head, row0, d_rows, group):
    n_dev, _, cols = gathered.shape
    n_tok = tokens.shape[0]
    k = group * d_rows
    gate_blk = row0 // d_rows
    return pl.pallas_call(
        draft_kernel,
        grid=(n_dev // group,),
        in_specs=[
            pl.BlockSpec((n_tok, k), lambda j: (0, j)),
            pl.BlockSpec((group, d_rows, cols), lambda j: (j, gate_blk, 0)),
            pl.BlockSpec((group, d_rows, cols), lambda j: (j, gate_blk + 1, 0)),
            pl.BlockSpec((1, cols), lambda j: (0, 0)),
        ],
        out_specs=pl.BlockSpec((n_tok, 1), lambda j: (0, 0)),
        out_shape=jax.ShapeDtypeStruct((n_tok, 1), jnp.float32),
        scratch_shapes=[
            pltpu.VMEM((n_tok, cols), jnp.float32),
            pltpu.VMEM((n_tok, cols), jnp.float32),
        ],
    )(tokens, gathered, gathered, head.reshape(1, cols))[:, 0]


def kv_kernel(x_ref, w_ref, out_ref):
    j = pl.program_id(0)

    @pl.when(j == 0)
    def _():
        out_ref[...] = jnp.zeros_like(out_ref)

    group, rows, _ = w_ref.shape
    acc = jnp.dot(x_ref[:, 0:rows], w_ref[0], preferred_element_type=jnp.float32)
    for i in range(1, group):
        acc += jnp.dot(
            x_ref[:, i * rows : (i + 1) * rows], w_ref[i], preferred_element_type=jnp.float32
        )
    out_ref[...] += acc


def kv_project(normed, gathered, v_rows, group):
    n_dev, _, cols = gathered.shape
    n_tok = normed.shape[0]
    k = group * v_rows
    return pl.pallas_call(
        kv_kernel,
        grid=(n_dev // group,),
        in_specs=[
            pl.BlockSpec((n_tok, k), lambda j: (0, j)),
            pl.BlockSpec((group, v_rows, cols), lambda j: (j, 0, 0)),
        ],
        out_specs=pl.BlockSpec((n_tok, cols), lambda j: (0, 0)),
        out_shape=jax.ShapeDtypeStruct((n_tok, cols), jnp.float32),
    )(normed, gathered)


def local(
    draft_tokens,
    draft_gate,
    draft_up,
    draft_head,
    verifier_rows,
    norm_gain,
    key_weight,
    value_weight,
    pool_query,
    flags,
    owner,
):
    seg_count = flags.shape[0]
    n_seq = lax.axis_size("seq")
    n_fsdp = lax.axis_size("fsdp")
    d_rows, d_cols = draft_gate.shape
    v_rows = key_weight.shape[0]
    kv_cols = key_weight.shape[1]
    kv_block = jnp.concatenate([key_weight, value_weight], axis=1)
    kv_block = kv_block.reshape(-1, d_cols)
    block = jnp.concatenate([kv_block, draft_gate, draft_up], axis=0)
    gathered = lax.all_gather(block, "fsdp", axis=0, tiled=False)
    kv_rows = kv_block.shape[0]

    normed = normalize_rows(verifier_rows, norm_gain)
    seg_kv = kv_project(normed, gathered, kv_rows, 8)
    seg_keys = seg_kv[:, :kv_cols]
    seg_values = seg_kv[:, kv_cols:]
    lane_pick = (
        owner[:, None] == jnp.arange(pool_query.shape[0], dtype=jnp.int32)[None, :]
    ).astype(jnp.float32)
    queries = jnp.einsum("sc,chd->shd", lane_pick, pool_query, precision=lax.Precision.HIGHEST)
    summary_key, summary_value = segment_pool(
        seg_keys.reshape(seg_count, SEGL, KVH, HD),
        seg_values.reshape(seg_count, SEGL, KVH, HD),
        queries,
        HD,
    )
    width = KVH * HD
    live_row = jnp.zeros((1, width), jnp.float32).at[0, :seg_count].set(flags.astype(jnp.float32))
    partial_scores = draft_scores(draft_tokens, gathered, draft_head, kv_rows, d_rows, 8)
    tail = jnp.concatenate(
        [
            partial_scores.reshape(-1, width),
            summary_key.reshape(seg_count, width),
            summary_value.reshape(seg_count, width),
            live_row,
        ],
        axis=0,
    )
    tail_all = jnp.stack(
        [tail]
        + [
            lax.ppermute(tail, "seq", [(i, (i + k) % n_seq) for i in range(n_seq)])
            for k in range(1, n_seq)
        ]
    )
    score_rows = partial_scores.shape[0] // width
    scores_all = tail_all[:, :score_rows].reshape(n_seq, -1)
    summary_all = tail_all[:, score_rows:]
    own = lax.axis_index("seq")
    own_tokens = seg_count * SEGL
    token_scores = jnp.sum(
        lax.dynamic_slice_in_dim(scores_all, own * own_tokens, own_tokens, axis=1), axis=0
    )
    draft_score = jnp.mean(token_scores.reshape(seg_count, SEGL), axis=1)
    key_all = summary_all[:, :seg_count].reshape(-1, KVH, HD)
    value_all = summary_all[:, seg_count : 2 * seg_count].reshape(-1, KVH, HD)
    live_all = summary_all[:, 2 * seg_count, :seg_count].reshape(-1)
    pooled = cross_pool(
        summary_key,
        key_all,
        value_all,
        live_all > 0.5,
        HD,
    )
    own_pooled = pooled.reshape(seg_count, KVH * HD)
    verdict = jnp.where(
        flags[:, None] == 1, jax.nn.sigmoid(draft_score)[:, None] * own_pooled, 0.0
    ).astype(jnp.bfloat16)
    return (draft_score, verdict)


def solution(mesh):
    return jax.shard_map(
        local,
        mesh=mesh,
        in_specs=(
            P("fsdp", None),
            P("fsdp", "seq"),
            P("fsdp", "seq"),
            P("seq"),
            P(("fsdp", "seq"), None),
            P(),
            P("fsdp", None),
            P("fsdp", None),
            P(),
            P(("fsdp", "seq")),
            P(("fsdp", "seq")),
        ),
        out_specs=(P(("fsdp", "seq")), P(("fsdp", "seq"), None)),
        check_vma=False,
    )
```

```python
import math

import jax
import jax.numpy as jnp
from jax import lax
from jax.experimental import pallas as pl
from jax.experimental.pallas import tpu as pltpu
from jax.sharding import PartitionSpec as P

KVH = 4
HD = 128
SEGL = 32


eps = 1e-05


def normalize_rows(rows, norm_gain):
    values = rows.astype(jnp.float32)
    scale = lax.rsqrt(jnp.mean(values * values, axis=-1, keepdims=True) + eps)
    return (values * scale * norm_gain).astype(jnp.bfloat16)


def segment_pool(seg_keys, seg_values, queries, head_size):
    scores = jnp.sum(seg_keys * queries[:, None], axis=-1) / math.sqrt(head_size)
    scores = scores - jnp.max(scores, axis=1, keepdims=True)
    weights = jnp.exp(scores)
    weights = weights / jnp.sum(weights, axis=1, keepdims=True)
    summary_key = jnp.sum(weights[..., None] * seg_keys, axis=1)
    summary_value = jnp.sum(weights[..., None] * seg_values, axis=1)
    return (summary_key, summary_value)


def cross_pool(query_keys, key_all, value_all, live_all, head_size):
    scores = jnp.sum(query_keys[:, :, None, :] * jnp.swapaxes(key_all, 0, 1)[None], axis=-1)
    scores = scores / math.sqrt(head_size)
    scores = jnp.where(live_all[None, None, :], scores, -1e30)
    highest = jnp.max(scores, axis=2, keepdims=True)
    weights = jnp.where(live_all[None, None, :], jnp.exp(scores - highest), 0.0)
    total = jnp.sum(weights, axis=2, keepdims=True)
    pooled = jnp.sum(weights[..., None] * jnp.swapaxes(value_all, 0, 1)[None], axis=2)
    return pooled / total


def draft_kernel(tok_ref, g_ref, u_ref, head_ref, out_ref, gacc, uacc):
    j = pl.program_id(0)

    @pl.when(j == 0)
    def _():
        gacc[...] = jnp.zeros_like(gacc)
        uacc[...] = jnp.zeros_like(uacc)

    t = tok_ref[...]
    k = g_ref.shape[0] * g_ref.shape[1]
    gacc[...] += jnp.dot(t, g_ref[...].reshape(k, -1), preferred_element_type=jnp.float32)
    uacc[...] += jnp.dot(t, u_ref[...].reshape(k, -1), preferred_element_type=jnp.float32)

    @pl.when(j == pl.num_programs(0) - 1)
    def _():
        g = gacc[...]
        act = g / (1.0 + jnp.exp(-g))
        col = jnp.sum(act * uacc[...] * head_ref[...], axis=1, keepdims=True)
        wide = jnp.broadcast_to(col, (col.shape[0], 128))
        out_ref[...] = jnp.transpose(wide)[0 : out_ref.shape[0], :]


def draft_scores(tokens, gathered, head, row0, d_rows, group):
    n_dev, _, cols = gathered.shape
    n_tok = tokens.shape[0]
    k = group * d_rows
    gate_blk = row0 // d_rows
    return pl.pallas_call(
        draft_kernel,
        grid=(n_dev // group,),
        in_specs=[
            pl.BlockSpec((n_tok, k), lambda j: (0, j)),
            pl.BlockSpec((group, d_rows, cols), lambda j: (j, gate_blk, 0)),
            pl.BlockSpec((group, d_rows, cols), lambda j: (j, gate_blk + 1, 0)),
            pl.BlockSpec((1, cols), lambda j: (0, 0)),
        ],
        out_specs=pl.BlockSpec((8, n_tok), lambda j: (0, 0)),
        out_shape=jax.ShapeDtypeStruct((8, n_tok), jnp.float32),
        scratch_shapes=[
            pltpu.VMEM((n_tok, cols), jnp.float32),
            pltpu.VMEM((n_tok, cols), jnp.float32),
        ],
    )(tokens, gathered, gathered, head.reshape(1, cols))[0]


def kv_kernel(x_ref, w_ref, out_ref):
    j = pl.program_id(0)

    @pl.when(j == 0)
    def _():
        out_ref[...] = jnp.zeros_like(out_ref)

    group, rows, _ = w_ref.shape
    acc = jnp.dot(x_ref[:, 0:rows], w_ref[0], preferred_element_type=jnp.float32)
    for i in range(1, group):
        acc += jnp.dot(
            x_ref[:, i * rows : (i + 1) * rows], w_ref[i], preferred_element_type=jnp.float32
        )
    out_ref[...] += acc


def kv_project(normed, gathered, v_rows, group):
    n_dev, _, cols = gathered.shape
    n_tok = normed.shape[0]
    k = group * v_rows
    return pl.pallas_call(
        kv_kernel,
        grid=(n_dev // group,),
        in_specs=[
            pl.BlockSpec((n_tok, k), lambda j: (0, j)),
            pl.BlockSpec((group, v_rows, cols), lambda j: (j, 0, 0)),
        ],
        out_specs=pl.BlockSpec((n_tok, cols), lambda j: (0, 0)),
        out_shape=jax.ShapeDtypeStruct((n_tok, cols), jnp.float32),
    )(normed, gathered)


def local(
    draft_tokens,
    draft_gate,
    draft_up,
    draft_head,
    verifier_rows,
    norm_gain,
    key_weight,
    value_weight,
    pool_query,
    flags,
    owner,
):
    seg_count = flags.shape[0]
    n_seq = lax.axis_size("seq")
    n_fsdp = lax.axis_size("fsdp")
    d_rows, d_cols = draft_gate.shape
    v_rows = key_weight.shape[0]
    kv_cols = key_weight.shape[1]
    kv_block = jnp.concatenate([key_weight, value_weight], axis=1)
    kv_block = kv_block.reshape(-1, d_cols)
    block = jnp.concatenate([kv_block, draft_gate, draft_up], axis=0)
    gathered = lax.all_gather(block, "fsdp", axis=0, tiled=False)
    kv_rows = kv_block.shape[0]

    normed = normalize_rows(verifier_rows, norm_gain)
    seg_kv = kv_project(normed, gathered, kv_rows, 8)
    seg_keys = seg_kv[:, :kv_cols]
    seg_values = seg_kv[:, kv_cols:]
    lane_pick = (
        owner[:, None] == jnp.arange(pool_query.shape[0], dtype=jnp.int32)[None, :]
    ).astype(jnp.float32)
    queries = jnp.einsum("sc,chd->shd", lane_pick, pool_query, precision=lax.Precision.HIGHEST)
    summary_key, summary_value = segment_pool(
        seg_keys.reshape(seg_count, SEGL, KVH, HD),
        seg_values.reshape(seg_count, SEGL, KVH, HD),
        queries,
        HD,
    )
    width = KVH * HD
    live_row = jnp.zeros((1, width), jnp.float32).at[0, :seg_count].set(flags.astype(jnp.float32))
    partial_scores = draft_scores(draft_tokens, gathered, draft_head, kv_rows, d_rows, 8)
    tail = jnp.concatenate(
        [
            partial_scores.reshape(-1, width),
            summary_key.reshape(seg_count, width),
            summary_value.reshape(seg_count, width),
            live_row,
        ],
        axis=0,
    )
    tail_all = tail[None]
    step = 1
    while step < n_seq:
        pairs = [(i, i ^ step) for i in range(n_seq)]
        tail_all = jnp.concatenate([tail_all, lax.ppermute(tail_all, "seq", pairs)], axis=0)
        step *= 2
    score_rows = partial_scores.shape[0] // width
    scores_all = tail_all[:, :score_rows].reshape(n_seq, -1)
    summary_all = tail_all[:, score_rows:]
    own = lax.axis_index("seq")
    own_tokens = seg_count * SEGL
    token_scores = jnp.sum(
        lax.dynamic_slice_in_dim(scores_all, own * own_tokens, own_tokens, axis=1), axis=0
    )
    draft_score = jnp.mean(token_scores.reshape(seg_count, SEGL), axis=1)
    key_all = summary_all[:, :seg_count].reshape(-1, KVH, HD)
    value_all = summary_all[:, seg_count : 2 * seg_count].reshape(-1, KVH, HD)
    live_all = summary_all[:, 2 * seg_count, :seg_count].reshape(-1)
    pooled = cross_pool(
        summary_key,
        key_all,
        value_all,
        live_all > 0.5,
        HD,
    )
    own_pooled = pooled.reshape(seg_count, KVH * HD)
    verdict = jnp.where(
        flags[:, None] == 1, jax.nn.sigmoid(draft_score)[:, None] * own_pooled, 0.0
    ).astype(jnp.bfloat16)
    return (draft_score, verdict)


def solution(mesh):
    return jax.shard_map(
        local,
        mesh=mesh,
        in_specs=(
            P("fsdp", None),
            P("fsdp", "seq"),
            P("fsdp", "seq"),
            P("seq"),
            P(("fsdp", "seq"), None),
            P(),
            P("fsdp", None),
            P("fsdp", None),
            P(),
            P(("fsdp", "seq")),
            P(("fsdp", "seq")),
        ),
        out_specs=(P(("fsdp", "seq")), P(("fsdp", "seq"), None)),
        check_vma=False,
    )
```

```python
import math

import jax
import jax.numpy as jnp
from jax import lax
from jax.experimental import pallas as pl
from jax.experimental.pallas import tpu as pltpu
from jax.sharding import PartitionSpec as P

KVH = 4
HD = 128
SEGL = 32


eps = 1e-05


def normalize_rows(rows, norm_gain):
    values = rows.astype(jnp.float32)
    scale = lax.rsqrt(jnp.mean(values * values, axis=-1, keepdims=True) + eps)
    return (values * scale * norm_gain).astype(jnp.bfloat16)


def segment_pool(seg_keys, seg_values, queries, head_size):
    scores = jnp.sum(seg_keys * queries[:, None], axis=-1) / math.sqrt(head_size)
    scores = scores - jnp.max(scores, axis=1, keepdims=True)
    weights = jnp.exp(scores)
    weights = weights / jnp.sum(weights, axis=1, keepdims=True)
    summary_key = jnp.sum(weights[..., None] * seg_keys, axis=1)
    summary_value = jnp.sum(weights[..., None] * seg_values, axis=1)
    return (summary_key, summary_value)


def cross_pool(query_keys, key_all, value_all, live_all, head_size):
    scores = jnp.sum(query_keys[:, :, None, :] * jnp.swapaxes(key_all, 0, 1)[None], axis=-1)
    scores = scores / math.sqrt(head_size)
    scores = jnp.where(live_all[None, None, :], scores, -1e30)
    highest = jnp.max(scores, axis=2, keepdims=True)
    weights = jnp.where(live_all[None, None, :], jnp.exp(scores - highest), 0.0)
    total = jnp.sum(weights, axis=2, keepdims=True)
    pooled = jnp.sum(weights[..., None] * jnp.swapaxes(value_all, 0, 1)[None], axis=2)
    return pooled / total


def fused_kernel(x_ref, w_ref, tok_ref, g_ref, u_ref, head_ref, kv_ref, score_ref, gacc, uacc):
    j = pl.program_id(0)

    @pl.when(j == 0)
    def _():
        kv_ref[...] = jnp.zeros_like(kv_ref)
        gacc[...] = jnp.zeros_like(gacc)
        uacc[...] = jnp.zeros_like(uacc)

    group, rows, _ = w_ref.shape
    acc = jnp.dot(x_ref[:, 0:rows], w_ref[0], preferred_element_type=jnp.float32)
    for i in range(1, group):
        acc += jnp.dot(
            x_ref[:, i * rows : (i + 1) * rows], w_ref[i], preferred_element_type=jnp.float32
        )
    kv_ref[...] += acc

    t = tok_ref[...]
    k = g_ref.shape[0] * g_ref.shape[1]
    gacc[...] += jnp.dot(t, g_ref[...].reshape(k, -1), preferred_element_type=jnp.float32)
    uacc[...] += jnp.dot(t, u_ref[...].reshape(k, -1), preferred_element_type=jnp.float32)

    @pl.when(j == pl.num_programs(0) - 1)
    def _():
        g = gacc[...]
        act = g / (1.0 + jnp.exp(-g))
        col = jnp.sum(act * uacc[...] * head_ref[...], axis=1, keepdims=True)
        wide = jnp.broadcast_to(col, (col.shape[0], 128))
        score_ref[...] = jnp.transpose(wide)[0 : score_ref.shape[0], :]


def project_all(normed, tokens, gathered, head, kv_rows, d_rows, steps):
    n_dev, _, cols = gathered.shape
    n_norm = normed.shape[0]
    n_tok = tokens.shape[0]
    group = n_dev // steps
    gate_blk = kv_rows // d_rows
    seg_kv, scores = pl.pallas_call(
        fused_kernel,
        grid=(steps,),
        in_specs=[
            pl.BlockSpec((n_norm, group * kv_rows), lambda j: (0, j)),
            pl.BlockSpec((group, kv_rows, cols), lambda j: (j, 0, 0)),
            pl.BlockSpec((n_tok, group * d_rows), lambda j: (0, j)),
            pl.BlockSpec((group, d_rows, cols), lambda j: (j, gate_blk, 0)),
            pl.BlockSpec((group, d_rows, cols), lambda j: (j, gate_blk + 1, 0)),
            pl.BlockSpec((1, cols), lambda j: (0, 0)),
        ],
        out_specs=[
            pl.BlockSpec((n_norm, cols), lambda j: (0, 0)),
            pl.BlockSpec((8, n_tok), lambda j: (0, 0)),
        ],
        out_shape=[
            jax.ShapeDtypeStruct((n_norm, cols), jnp.float32),
            jax.ShapeDtypeStruct((8, n_tok), jnp.float32),
        ],
        scratch_shapes=[
            pltpu.VMEM((n_tok, cols), jnp.float32),
            pltpu.VMEM((n_tok, cols), jnp.float32),
        ],
    )(normed, gathered, tokens, gathered, gathered, head.reshape(1, cols))
    return seg_kv, scores[0]


def local(
    draft_tokens,
    draft_gate,
    draft_up,
    draft_head,
    verifier_rows,
    norm_gain,
    key_weight,
    value_weight,
    pool_query,
    flags,
    owner,
):
    seg_count = flags.shape[0]
    n_seq = lax.axis_size("seq")
    n_fsdp = lax.axis_size("fsdp")
    d_rows, d_cols = draft_gate.shape
    v_rows = key_weight.shape[0]
    kv_cols = key_weight.shape[1]
    kv_block = jnp.concatenate([key_weight, value_weight], axis=1)
    kv_block = kv_block.reshape(-1, d_cols)
    block = jnp.concatenate([kv_block, draft_gate, draft_up], axis=0)
    gathered = lax.all_gather(block, "fsdp", axis=0, tiled=False)
    kv_rows = kv_block.shape[0]

    normed = normalize_rows(verifier_rows, norm_gain)
    seg_kv, partial_scores = project_all(
        normed, draft_tokens, gathered, draft_head, kv_rows, d_rows, 4
    )
    seg_keys = seg_kv[:, :kv_cols]
    seg_values = seg_kv[:, kv_cols:]
    lane_pick = (
        owner[:, None] == jnp.arange(pool_query.shape[0], dtype=jnp.int32)[None, :]
    ).astype(jnp.float32)
    queries = jnp.einsum("sc,chd->shd", lane_pick, pool_query, precision=lax.Precision.HIGHEST)
    summary_key, summary_value = segment_pool(
        seg_keys.reshape(seg_count, SEGL, KVH, HD),
        seg_values.reshape(seg_count, SEGL, KVH, HD),
        queries,
        HD,
    )
    width = KVH * HD
    live_row = jnp.zeros((1, width), jnp.float32).at[0, :seg_count].set(flags.astype(jnp.float32))
    tail = jnp.concatenate(
        [
            partial_scores.reshape(-1, width),
            summary_key.reshape(seg_count, width),
            summary_value.reshape(seg_count, width),
            live_row,
        ],
        axis=0,
    )
    tail_all = jnp.stack(
        [tail]
        + [
            lax.ppermute(tail, "seq", [(i, (i + k) % n_seq) for i in range(n_seq)])
            for k in range(1, n_seq)
        ]
    )
    score_rows = partial_scores.shape[0] // width
    scores_all = tail_all[:, :score_rows].reshape(n_seq, -1)
    summary_all = tail_all[:, score_rows:]
    own = lax.axis_index("seq")
    own_tokens = seg_count * SEGL
    token_scores = jnp.sum(
        lax.dynamic_slice_in_dim(scores_all, own * own_tokens, own_tokens, axis=1), axis=0
    )
    draft_score = jnp.mean(token_scores.reshape(seg_count, SEGL), axis=1)
    key_all = summary_all[:, :seg_count].reshape(-1, KVH, HD)
    value_all = summary_all[:, seg_count : 2 * seg_count].reshape(-1, KVH, HD)
    live_all = summary_all[:, 2 * seg_count, :seg_count].reshape(-1)
    pooled = cross_pool(
        summary_key,
        key_all,
        value_all,
        live_all > 0.5,
        HD,
    )
    own_pooled = pooled.reshape(seg_count, KVH * HD)
    verdict = jnp.where(
        flags[:, None] == 1, jax.nn.sigmoid(draft_score)[:, None] * own_pooled, 0.0
    ).astype(jnp.bfloat16)
    return (draft_score, verdict)


def solution(mesh):
    return jax.shard_map(
        local,
        mesh=mesh,
        in_specs=(
            P("fsdp", None),
            P("fsdp", "seq"),
            P("fsdp", "seq"),
            P("seq"),
            P(("fsdp", "seq"), None),
            P(),
            P("fsdp", None),
            P("fsdp", None),
            P(),
            P(("fsdp", "seq")),
            P(("fsdp", "seq")),
        ),
        out_specs=(P(("fsdp", "seq")), P(("fsdp", "seq"), None)),
        check_vma=False,
    )
```

```python
import math

import jax
import jax.numpy as jnp
from jax import lax
from jax.experimental import pallas as pl
from jax.experimental.pallas import tpu as pltpu
from jax.sharding import PartitionSpec as P

KVH = 4
HD = 128
SEGL = 32


eps = 1e-05


def normalize_rows(rows, norm_gain):
    values = rows.astype(jnp.float32)
    scale = lax.rsqrt(jnp.mean(values * values, axis=-1, keepdims=True) + eps)
    return (values * scale * norm_gain).astype(jnp.bfloat16)


def segment_pool(seg_keys, seg_values, queries, head_size):
    scores = jnp.sum(seg_keys * queries[:, None], axis=-1) / math.sqrt(head_size)
    scores = scores - jnp.max(scores, axis=1, keepdims=True)
    weights = jnp.exp(scores)
    weights = weights / jnp.sum(weights, axis=1, keepdims=True)
    summary_key = jnp.sum(weights[..., None] * seg_keys, axis=1)
    summary_value = jnp.sum(weights[..., None] * seg_values, axis=1)
    return (summary_key, summary_value)


def cross_pool(query_keys, key_all, value_all, live_all, head_size):
    scores = jnp.sum(query_keys[:, :, None, :] * jnp.swapaxes(key_all, 0, 1)[None], axis=-1)
    scores = scores / math.sqrt(head_size)
    scores = jnp.where(live_all[None, None, :], scores, -1e30)
    highest = jnp.max(scores, axis=2, keepdims=True)
    weights = jnp.where(live_all[None, None, :], jnp.exp(scores - highest), 0.0)
    total = jnp.sum(weights, axis=2, keepdims=True)
    pooled = jnp.sum(weights[..., None] * jnp.swapaxes(value_all, 0, 1)[None], axis=2)
    return pooled / total


def fused_kernel(
    x_ref, k_ref, v_ref, tok_ref, glo_ref, ghi_ref, ulo_ref, uhi_ref, head_ref,
    kv_ref, score_ref, gacc, uacc,
):
    j = pl.program_id(0)

    @pl.when(j == 0)
    def _():
        kv_ref[...] = jnp.zeros_like(kv_ref)
        gacc[...] = jnp.zeros_like(gacc)
        uacc[...] = jnp.zeros_like(uacc)

    def blocks_dot(x, w_ref):
        group, rows, _ = w_ref.shape
        acc = jnp.dot(x[:, 0:rows], w_ref[0], preferred_element_type=jnp.float32)
        for i in range(1, group):
            acc += jnp.dot(x[:, i * rows : (i + 1) * rows], w_ref[i], preferred_element_type=jnp.float32)
        return acc

    half = k_ref.shape[2]
    x = x_ref[...]
    kv_ref[:, 0:half] += blocks_dot(x, k_ref)
    kv_ref[:, half:] += blocks_dot(x, v_ref)

    t = tok_ref[...]
    k = glo_ref.shape[0] * glo_ref.shape[1]
    dh = glo_ref.shape[2]

    def flat_dot(w_ref):
        return jnp.dot(t, w_ref[...].reshape(k, -1), preferred_element_type=jnp.float32)

    gacc[:, 0:dh] += flat_dot(glo_ref)
    gacc[:, dh:] += flat_dot(ghi_ref)
    uacc[:, 0:dh] += flat_dot(ulo_ref)
    uacc[:, dh:] += flat_dot(uhi_ref)

    @pl.when(j == pl.num_programs(0) - 1)
    def _():
        g = gacc[...]
        act = g / (1.0 + jnp.exp(-g))
        col = jnp.sum(act * uacc[...] * head_ref[...], axis=1, keepdims=True)
        wide = jnp.broadcast_to(col, (col.shape[0], 128))
        score_ref[...] = jnp.transpose(wide)[0 : score_ref.shape[0], :]


def project_all(normed, tokens, gathered, head, kv_rows, d_rows, steps):
    n_dev, _, half = gathered.shape
    n_norm = normed.shape[0]
    n_tok = tokens.shape[0]
    group = n_dev // steps
    g0 = 2 * kv_rows // d_rows
    w_spec = lambda row_blk: pl.BlockSpec((group, kv_rows, half), lambda j: (j, row_blk, 0))
    d_spec = lambda row_blk: pl.BlockSpec((group, d_rows, half), lambda j: (j, row_blk, 0))
    seg_kv, scores = pl.pallas_call(
        fused_kernel,
        grid=(steps,),
        in_specs=[
            pl.BlockSpec((n_norm, group * kv_rows), lambda j: (0, j)),
            w_spec(0),
            w_spec(1),
            pl.BlockSpec((n_tok, group * d_rows), lambda j: (0, j)),
            d_spec(g0),
            d_spec(g0 + 1),
            d_spec(g0 + 2),
            d_spec(g0 + 3),
            pl.BlockSpec((1, 2 * half), lambda j: (0, 0)),
        ],
        out_specs=[
            pl.BlockSpec((n_norm, 2 * half), lambda j: (0, 0)),
            pl.BlockSpec((8, n_tok), lambda j: (0, 0)),
        ],
        out_shape=[
            jax.ShapeDtypeStruct((n_norm, 2 * half), jnp.float32),
            jax.ShapeDtypeStruct((8, n_tok), jnp.float32),
        ],
        scratch_shapes=[
            pltpu.VMEM((n_tok, 2 * half), jnp.float32),
            pltpu.VMEM((n_tok, 2 * half), jnp.float32),
        ],
    )(normed, gathered, gathered, tokens, gathered, gathered, gathered, gathered, head.reshape(1, -1))
    return seg_kv, scores[0]


def local(
    draft_tokens,
    draft_gate,
    draft_up,
    draft_head,
    verifier_rows,
    norm_gain,
    key_weight,
    value_weight,
    pool_query,
    flags,
    owner,
):
    seg_count = flags.shape[0]
    n_seq = lax.axis_size("seq")
    n_fsdp = lax.axis_size("fsdp")
    d_rows, d_cols = draft_gate.shape
    v_rows = key_weight.shape[0]
    kv_cols = key_weight.shape[1]
    dh = d_cols // 2
    block = jnp.concatenate(
        [
            key_weight,
            value_weight,
            draft_gate[:, :dh],
            draft_gate[:, dh:],
            draft_up[:, :dh],
            draft_up[:, dh:],
        ],
        axis=0,
    )
    gathered = lax.all_gather(block, "fsdp", axis=0, tiled=False)
    kv_rows = v_rows

    normed = normalize_rows(verifier_rows, norm_gain)
    seg_kv, partial_scores = project_all(
        normed, draft_tokens, gathered, draft_head, kv_rows, d_rows, 4
    )
    seg_keys = seg_kv[:, :kv_cols]
    seg_values = seg_kv[:, kv_cols:]
    lane_pick = (
        owner[:, None] == jnp.arange(pool_query.shape[0], dtype=jnp.int32)[None, :]
    ).astype(jnp.float32)
    queries = jnp.einsum("sc,chd->shd", lane_pick, pool_query, precision=lax.Precision.HIGHEST)
    summary_key, summary_value = segment_pool(
        seg_keys.reshape(seg_count, SEGL, KVH, HD),
        seg_values.reshape(seg_count, SEGL, KVH, HD),
        queries,
        HD,
    )
    width = KVH * HD
    live_row = jnp.zeros((1, width), jnp.float32).at[0, :seg_count].set(flags.astype(jnp.float32))
    tail = jnp.concatenate(
        [
            partial_scores.reshape(-1, width),
            summary_key.reshape(seg_count, width),
            summary_value.reshape(seg_count, width),
            live_row,
        ],
        axis=0,
    )
    tail_all = jnp.stack(
        [tail]
        + [
            lax.ppermute(tail, "seq", [(i, (i + k) % n_seq) for i in range(n_seq)])
            for k in range(1, n_seq)
        ]
    )
    score_rows = partial_scores.shape[0] // width
    scores_all = tail_all[:, :score_rows].reshape(n_seq, -1)
    summary_all = tail_all[:, score_rows:]
    own = lax.axis_index("seq")
    own_tokens = seg_count * SEGL
    token_scores = jnp.sum(
        lax.dynamic_slice_in_dim(scores_all, own * own_tokens, own_tokens, axis=1), axis=0
    )
    draft_score = jnp.mean(token_scores.reshape(seg_count, SEGL), axis=1)
    key_all = summary_all[:, :seg_count].reshape(-1, KVH, HD)
    value_all = summary_all[:, seg_count : 2 * seg_count].reshape(-1, KVH, HD)
    live_all = summary_all[:, 2 * seg_count, :seg_count].reshape(-1)
    pooled = cross_pool(
        summary_key,
        key_all,
        value_all,
        live_all > 0.5,
        HD,
    )
    own_pooled = pooled.reshape(seg_count, KVH * HD)
    verdict = jnp.where(
        flags[:, None] == 1, jax.nn.sigmoid(draft_score)[:, None] * own_pooled, 0.0
    ).astype(jnp.bfloat16)
    return (draft_score, verdict)


def solution(mesh):
    return jax.shard_map(
        local,
        mesh=mesh,
        in_specs=(
            P("fsdp", None),
            P("fsdp", "seq"),
            P("fsdp", "seq"),
            P("seq"),
            P(("fsdp", "seq"), None),
            P(),
            P("fsdp", None),
            P("fsdp", None),
            P(),
            P(("fsdp", "seq")),
            P(("fsdp", "seq")),
        ),
        out_specs=(P(("fsdp", "seq")), P(("fsdp", "seq"), None)),
        check_vma=False,
    )
```

```python
import math

import jax
import jax.numpy as jnp
from jax import lax
from jax.experimental import pallas as pl
from jax.experimental.pallas import tpu as pltpu
from jax.sharding import PartitionSpec as P

KVH = 4
HD = 128
SEGL = 32


eps = 1e-05


def normalize_rows(rows, norm_gain):
    values = rows.astype(jnp.float32)
    scale = lax.rsqrt(jnp.mean(values * values, axis=-1, keepdims=True) + eps)
    return (values * scale * norm_gain).astype(jnp.bfloat16)


def segment_pool(seg_keys, seg_values, queries, head_size):
    scores = jnp.sum(seg_keys * queries[:, None], axis=-1) / math.sqrt(head_size)
    scores = scores - jnp.max(scores, axis=1, keepdims=True)
    weights = jnp.exp(scores)
    weights = weights / jnp.sum(weights, axis=1, keepdims=True)
    summary_key = jnp.sum(weights[..., None] * seg_keys, axis=1)
    summary_value = jnp.sum(weights[..., None] * seg_values, axis=1)
    return (summary_key, summary_value)


def cross_pool(query_keys, key_all, value_all, live_all, head_size):
    scores = jnp.sum(query_keys[:, :, None, :] * jnp.swapaxes(key_all, 0, 1)[None], axis=-1)
    scores = scores / math.sqrt(head_size)
    scores = jnp.where(live_all[None, None, :], scores, -1e30)
    highest = jnp.max(scores, axis=2, keepdims=True)
    weights = jnp.where(live_all[None, None, :], jnp.exp(scores - highest), 0.0)
    total = jnp.sum(weights, axis=2, keepdims=True)
    pooled = jnp.sum(weights[..., None] * jnp.swapaxes(value_all, 0, 1)[None], axis=2)
    return pooled / total


def fused_kernel(x_ref, w_ref, tok_ref, g_ref, u_ref, head_ref, kv_ref, score_ref, gacc, uacc):
    j = pl.program_id(0)

    @pl.when(j == 0)
    def _():
        kv_ref[...] = jnp.zeros_like(kv_ref)
        gacc[...] = jnp.zeros_like(gacc)
        uacc[...] = jnp.zeros_like(uacc)

    group, rows, _ = w_ref.shape
    acc = jnp.dot(x_ref[:, 0:rows], w_ref[0], preferred_element_type=jnp.float32)
    for i in range(1, group):
        acc += jnp.dot(
            x_ref[:, i * rows : (i + 1) * rows], w_ref[i], preferred_element_type=jnp.float32
        )
    kv_ref[...] += acc

    t = tok_ref[...]
    k = g_ref.shape[0] * g_ref.shape[1]
    gacc[...] += jnp.dot(t, g_ref[...].reshape(k, -1), preferred_element_type=jnp.float32)
    uacc[...] += jnp.dot(t, u_ref[...].reshape(k, -1), preferred_element_type=jnp.float32)

    @pl.when(j == pl.num_programs(0) - 1)
    def _():
        g = gacc[...]
        act = g / (1.0 + jnp.exp(-g))
        col = jnp.sum(act * uacc[...] * head_ref[...], axis=1, keepdims=True)
        wide = jnp.broadcast_to(col, (col.shape[0], 128))
        score_ref[...] = jnp.transpose(wide)[0 : score_ref.shape[0], :]


def project_all(normed, tokens, gathered, head, kv_rows, d_rows, steps):
    n_dev, _, cols = gathered.shape
    n_norm = normed.shape[0]
    n_tok = tokens.shape[0]
    group = n_dev // steps
    gate_blk = kv_rows // d_rows
    seg_kv, scores = pl.pallas_call(
        fused_kernel,
        grid=(steps,),
        in_specs=[
            pl.BlockSpec((n_norm, group * kv_rows), lambda j: (0, j)),
            pl.BlockSpec((group, kv_rows, cols), lambda j: (j, 0, 0)),
            pl.BlockSpec((n_tok, group * d_rows), lambda j: (0, j)),
            pl.BlockSpec((group, d_rows, cols), lambda j: (j, gate_blk, 0)),
            pl.BlockSpec((group, d_rows, cols), lambda j: (j, gate_blk + 1, 0)),
            pl.BlockSpec((1, cols), lambda j: (0, 0)),
        ],
        out_specs=[
            pl.BlockSpec((n_norm, cols), lambda j: (0, 0)),
            pl.BlockSpec((8, n_tok), lambda j: (0, 0)),
        ],
        out_shape=[
            jax.ShapeDtypeStruct((n_norm, cols), jnp.float32),
            jax.ShapeDtypeStruct((8, n_tok), jnp.float32),
        ],
        scratch_shapes=[
            pltpu.VMEM((n_tok, cols), jnp.float32),
            pltpu.VMEM((n_tok, cols), jnp.float32),
        ],
    )(normed, gathered, tokens, gathered, gathered, head.reshape(1, cols))
    return seg_kv, scores[0]


def pack_kernel(k_hbm, v_hbm, g_hbm, u_hbm, out_hbm, sems):
    rows, half = k_hbm.shape
    d_rows = g_hbm.shape[0]
    copies = [
        pltpu.make_async_copy(k_hbm, out_hbm.at[0:rows, 0:half], sems.at[0]),
        pltpu.make_async_copy(v_hbm, out_hbm.at[0:rows, half : 2 * half], sems.at[1]),
        pltpu.make_async_copy(g_hbm, out_hbm.at[rows : rows + d_rows, :], sems.at[2]),
        pltpu.make_async_copy(u_hbm, out_hbm.at[rows + d_rows : rows + 2 * d_rows, :], sems.at[3]),
    ]
    for c in copies:
        c.start()
    for c in copies:
        c.wait()


def pack_block(key_weight, value_weight, draft_gate, draft_up):
    rows, half = key_weight.shape
    d_rows, cols = draft_gate.shape
    any_spec = pl.BlockSpec(memory_space=pl.ANY)
    return pl.pallas_call(
        pack_kernel,
        in_specs=[any_spec] * 4,
        out_specs=any_spec,
        out_shape=jax.ShapeDtypeStruct((rows + 2 * d_rows, cols), key_weight.dtype),
        scratch_shapes=[pltpu.SemaphoreType.DMA((4,))],
    )(key_weight, value_weight, draft_gate, draft_up)


def local(
    draft_tokens,
    draft_gate,
    draft_up,
    draft_head,
    verifier_rows,
    norm_gain,
    key_weight,
    value_weight,
    pool_query,
    flags,
    owner,
):
    seg_count = flags.shape[0]
    n_seq = lax.axis_size("seq")
    n_fsdp = lax.axis_size("fsdp")
    d_rows, d_cols = draft_gate.shape
    v_rows = key_weight.shape[0]
    kv_cols = key_weight.shape[1]
    block = pack_block(key_weight, value_weight, draft_gate, draft_up)
    gathered = lax.all_gather(block, "fsdp", axis=0, tiled=False)
    kv_rows = key_weight.shape[0]

    normed = normalize_rows(verifier_rows, norm_gain)
    seg_kv, partial_scores = project_all(
        normed, draft_tokens, gathered, draft_head, kv_rows, d_rows, 4
    )
    seg_keys = seg_kv[:, :kv_cols]
    seg_values = seg_kv[:, kv_cols:]
    lane_pick = (
        owner[:, None] == jnp.arange(pool_query.shape[0], dtype=jnp.int32)[None, :]
    ).astype(jnp.float32)
    queries = jnp.einsum("sc,chd->shd", lane_pick, pool_query, precision=lax.Precision.HIGHEST)
    summary_key, summary_value = segment_pool(
        seg_keys.reshape(seg_count, SEGL, KVH, HD),
        seg_values.reshape(seg_count, SEGL, KVH, HD),
        queries,
        HD,
    )
    width = KVH * HD
    live_row = jnp.zeros((1, width), jnp.float32).at[0, :seg_count].set(flags.astype(jnp.float32))
    tail = jnp.concatenate(
        [
            partial_scores.reshape(-1, width),
            summary_key.reshape(seg_count, width),
            summary_value.reshape(seg_count, width),
            live_row,
        ],
        axis=0,
    )
    tail_all = jnp.stack(
        [tail]
        + [
            lax.ppermute(tail, "seq", [(i, (i + k) % n_seq) for i in range(n_seq)])
            for k in range(1, n_seq)
        ]
    )
    score_rows = partial_scores.shape[0] // width
    scores_all = tail_all[:, :score_rows].reshape(n_seq, -1)
    summary_all = tail_all[:, score_rows:]
    own = lax.axis_index("seq")
    own_tokens = seg_count * SEGL
    token_scores = jnp.sum(
        lax.dynamic_slice_in_dim(scores_all, own * own_tokens, own_tokens, axis=1), axis=0
    )
    draft_score = jnp.mean(token_scores.reshape(seg_count, SEGL), axis=1)
    key_all = summary_all[:, :seg_count].reshape(-1, KVH, HD)
    value_all = summary_all[:, seg_count : 2 * seg_count].reshape(-1, KVH, HD)
    live_all = summary_all[:, 2 * seg_count, :seg_count].reshape(-1)
    pooled = cross_pool(
        summary_key,
        key_all,
        value_all,
        live_all > 0.5,
        HD,
    )
    own_pooled = pooled.reshape(seg_count, KVH * HD)
    verdict = jnp.where(
        flags[:, None] == 1, jax.nn.sigmoid(draft_score)[:, None] * own_pooled, 0.0
    ).astype(jnp.bfloat16)
    return (draft_score, verdict)


def solution(mesh):
    return jax.shard_map(
        local,
        mesh=mesh,
        in_specs=(
            P("fsdp", None),
            P("fsdp", "seq"),
            P("fsdp", "seq"),
            P("seq"),
            P(("fsdp", "seq"), None),
            P(),
            P("fsdp", None),
            P("fsdp", None),
            P(),
            P(("fsdp", "seq")),
            P(("fsdp", "seq")),
        ),
        out_specs=(P(("fsdp", "seq")), P(("fsdp", "seq"), None)),
        check_vma=False,
    )
```

```python
import math

import jax
import jax.numpy as jnp
from jax import lax
from jax.experimental import pallas as pl
from jax.experimental.pallas import tpu as pltpu
from jax.sharding import PartitionSpec as P

KVH = 4
HD = 128
SEGL = 32


eps = 1e-05


def normalize_rows(rows, norm_gain):
    values = rows.astype(jnp.float32)
    scale = lax.rsqrt(jnp.mean(values * values, axis=-1, keepdims=True) + eps)
    return (values * scale * norm_gain).astype(jnp.bfloat16)


def segment_pool(seg_keys, seg_values, queries, head_size):
    scores = jnp.sum(seg_keys * queries[:, None], axis=-1) / math.sqrt(head_size)
    scores = scores - jnp.max(scores, axis=1, keepdims=True)
    weights = jnp.exp(scores)
    weights = weights / jnp.sum(weights, axis=1, keepdims=True)
    summary_key = jnp.sum(weights[..., None] * seg_keys, axis=1)
    summary_value = jnp.sum(weights[..., None] * seg_values, axis=1)
    return (summary_key, summary_value)


def cross_pool(query_keys, key_all, value_all, live_all, head_size):
    scores = jnp.sum(query_keys[:, :, None, :] * jnp.swapaxes(key_all, 0, 1)[None], axis=-1)
    scores = scores / math.sqrt(head_size)
    scores = jnp.where(live_all[None, None, :], scores, -1e30)
    highest = jnp.max(scores, axis=2, keepdims=True)
    weights = jnp.where(live_all[None, None, :], jnp.exp(scores - highest), 0.0)
    total = jnp.sum(weights, axis=2, keepdims=True)
    pooled = jnp.sum(weights[..., None] * jnp.swapaxes(value_all, 0, 1)[None], axis=2)
    return pooled / total


def fused_kernel(
    x_ref, w_ref, tok_ref, g_ref, u_ref, head_ref, q_ref, live_ref, tail_ref, kv_ref, gacc, uacc
):
    j = pl.program_id(0)

    @pl.when(j == 0)
    def _():
        kv_ref[...] = jnp.zeros_like(kv_ref)
        gacc[...] = jnp.zeros_like(gacc)
        uacc[...] = jnp.zeros_like(uacc)

    group, rows, _ = w_ref.shape
    acc = jnp.dot(x_ref[:, 0:rows], w_ref[0], preferred_element_type=jnp.float32)
    for i in range(1, group):
        acc += jnp.dot(
            x_ref[:, i * rows : (i + 1) * rows], w_ref[i], preferred_element_type=jnp.float32
        )
    kv_ref[...] += acc

    t = tok_ref[...]
    k = g_ref.shape[0] * g_ref.shape[1]
    gacc[...] += jnp.dot(t, g_ref[...].reshape(k, -1), preferred_element_type=jnp.float32)
    uacc[...] += jnp.dot(t, u_ref[...].reshape(k, -1), preferred_element_type=jnp.float32)

    @pl.when(j == pl.num_programs(0) - 1)
    def _():
        g = gacc[...]
        act = g / (1.0 + jnp.exp(-g))
        col = jnp.sum(act * uacc[...] * head_ref[...], axis=1, keepdims=True)
        wide = jnp.broadcast_to(col, (col.shape[0], 128))
        row = jnp.transpose(wide)[0:1, :]
        width = tail_ref.shape[1]
        score_rows = row.shape[1] // width
        for r in range(score_rows):
            tail_ref[r : r + 1, :] = row[:, r * width : (r + 1) * width]
        segs = q_ref.shape[0]
        kv = kv_ref[...]
        keys = kv[:, 0:width].reshape(segs, -1, width)
        values = kv[:, width:].reshape(segs, -1, width)
        prod = keys * q_ref[...]
        for h in range(width // HD):
            lanes = slice(h * HD, (h + 1) * HD)
            sc = jnp.sum(prod[:, :, lanes], axis=2, keepdims=True) / math.sqrt(HD)
            sc = sc - jnp.max(sc, axis=1, keepdims=True)
            wt = jnp.exp(sc)
            wt = wt / jnp.sum(wt, axis=1, keepdims=True)
            r0 = score_rows
            tail_ref[r0 : r0 + segs, lanes] = jnp.sum(wt * keys[:, :, lanes], axis=1)
            r0 = score_rows + segs
            tail_ref[r0 : r0 + segs, lanes] = jnp.sum(wt * values[:, :, lanes], axis=1)
        tail_ref[score_rows + 2 * segs :, :] = live_ref[...]


def project_all(normed, tokens, gathered, head, queries, live_row, kv_rows, d_rows, steps):
    n_dev, _, cols = gathered.shape
    n_norm = normed.shape[0]
    n_tok = tokens.shape[0]
    segs = queries.shape[0]
    width = queries.shape[2]
    tail_rows = n_tok // width + 2 * segs + 1
    group = n_dev // steps
    gate_blk = kv_rows // d_rows
    return pl.pallas_call(
        fused_kernel,
        grid=(steps,),
        in_specs=[
            pl.BlockSpec((n_norm, group * kv_rows), lambda j: (0, j)),
            pl.BlockSpec((group, kv_rows, cols), lambda j: (j, 0, 0)),
            pl.BlockSpec((n_tok, group * d_rows), lambda j: (0, j)),
            pl.BlockSpec((group, d_rows, cols), lambda j: (j, gate_blk, 0)),
            pl.BlockSpec((group, d_rows, cols), lambda j: (j, gate_blk + 1, 0)),
            pl.BlockSpec((1, cols), lambda j: (0, 0)),
            pl.BlockSpec(queries.shape, lambda j: (0, 0, 0)),
            pl.BlockSpec(live_row.shape, lambda j: (0, 0)),
        ],
        out_specs=pl.BlockSpec((tail_rows, width), lambda j: (0, 0)),
        out_shape=jax.ShapeDtypeStruct((tail_rows, width), jnp.float32),
        scratch_shapes=[
            pltpu.VMEM((n_norm, cols), jnp.float32),
            pltpu.VMEM((n_tok, cols), jnp.float32),
            pltpu.VMEM((n_tok, cols), jnp.float32),
        ],
    )(normed, gathered, tokens, gathered, gathered, head.reshape(1, cols), queries, live_row)


def local(
    draft_tokens,
    draft_gate,
    draft_up,
    draft_head,
    verifier_rows,
    norm_gain,
    key_weight,
    value_weight,
    pool_query,
    flags,
    owner,
):
    seg_count = flags.shape[0]
    n_seq = lax.axis_size("seq")
    n_fsdp = lax.axis_size("fsdp")
    d_rows, d_cols = draft_gate.shape
    v_rows = key_weight.shape[0]
    kv_cols = key_weight.shape[1]
    kv_block = jnp.concatenate([key_weight, value_weight], axis=1)
    kv_block = kv_block.reshape(-1, d_cols)
    block = jnp.concatenate([kv_block, draft_gate, draft_up], axis=0)
    gathered = lax.all_gather(block, "fsdp", axis=0, tiled=False)
    kv_rows = kv_block.shape[0]

    normed = normalize_rows(verifier_rows, norm_gain)
    lane_pick = (
        owner[:, None] == jnp.arange(pool_query.shape[0], dtype=jnp.int32)[None, :]
    ).astype(jnp.float32)
    queries = jnp.einsum("sc,chd->shd", lane_pick, pool_query, precision=lax.Precision.HIGHEST)
    width = KVH * HD
    live_row = jnp.zeros((1, width), jnp.float32).at[0, :seg_count].set(flags.astype(jnp.float32))
    tail = project_all(
        normed,
        draft_tokens,
        gathered,
        draft_head,
        queries.reshape(seg_count, 1, width),
        live_row,
        kv_rows,
        d_rows,
        4,
    )
    score_rows = draft_tokens.shape[0] // width
    summary_key = tail[score_rows : score_rows + seg_count].reshape(seg_count, KVH, HD)
    tail_all = jnp.stack(
        [tail]
        + [
            lax.ppermute(tail, "seq", [(i, (i + k) % n_seq) for i in range(n_seq)])
            for k in range(1, n_seq)
        ]
    )
    scores_all = tail_all[:, :score_rows].reshape(n_seq, -1)
    summary_all = tail_all[:, score_rows:]
    own = lax.axis_index("seq")
    own_tokens = seg_count * SEGL
    token_scores = jnp.sum(
        lax.dynamic_slice_in_dim(scores_all, own * own_tokens, own_tokens, axis=1), axis=0
    )
    draft_score = jnp.mean(token_scores.reshape(seg_count, SEGL), axis=1)
    key_all = summary_all[:, :seg_count].reshape(-1, KVH, HD)
    value_all = summary_all[:, seg_count : 2 * seg_count].reshape(-1, KVH, HD)
    live_all = summary_all[:, 2 * seg_count, :seg_count].reshape(-1)
    pooled = cross_pool(
        summary_key,
        key_all,
        value_all,
        live_all > 0.5,
        HD,
    )
    own_pooled = pooled.reshape(seg_count, KVH * HD)
    verdict = jnp.where(
        flags[:, None] == 1, jax.nn.sigmoid(draft_score)[:, None] * own_pooled, 0.0
    ).astype(jnp.bfloat16)
    return (draft_score, verdict)


def solution(mesh):
    return jax.shard_map(
        local,
        mesh=mesh,
        in_specs=(
            P("fsdp", None),
            P("fsdp", "seq"),
            P("fsdp", "seq"),
            P("seq"),
            P(("fsdp", "seq"), None),
            P(),
            P("fsdp", None),
            P("fsdp", None),
            P(),
            P(("fsdp", "seq")),
            P(("fsdp", "seq")),
        ),
        out_specs=(P(("fsdp", "seq")), P(("fsdp", "seq"), None)),
        check_vma=False,
    )
```

```python
import math

import jax
import jax.numpy as jnp
from jax import lax
from jax.experimental import pallas as pl
from jax.experimental.pallas import tpu as pltpu
from jax.sharding import PartitionSpec as P

KVH = 4
HD = 128
SEGL = 32


eps = 1e-05


def normalize_rows(rows, norm_gain):
    values = rows.astype(jnp.float32)
    scale = lax.rsqrt(jnp.mean(values * values, axis=-1, keepdims=True) + eps)
    return (values * scale * norm_gain).astype(jnp.bfloat16)


def segment_pool(seg_keys, seg_values, queries, head_size):
    scores = jnp.sum(seg_keys * queries[:, None], axis=-1) / math.sqrt(head_size)
    scores = scores - jnp.max(scores, axis=1, keepdims=True)
    weights = jnp.exp(scores)
    weights = weights / jnp.sum(weights, axis=1, keepdims=True)
    summary_key = jnp.sum(weights[..., None] * seg_keys, axis=1)
    summary_value = jnp.sum(weights[..., None] * seg_values, axis=1)
    return (summary_key, summary_value)


def cross_pool(query_keys, key_all, value_all, live_all, head_size):
    scores = jnp.sum(query_keys[:, :, None, :] * jnp.swapaxes(key_all, 0, 1)[None], axis=-1)
    scores = scores / math.sqrt(head_size)
    scores = jnp.where(live_all[None, None, :], scores, -1e30)
    highest = jnp.max(scores, axis=2, keepdims=True)
    weights = jnp.where(live_all[None, None, :], jnp.exp(scores - highest), 0.0)
    total = jnp.sum(weights, axis=2, keepdims=True)
    pooled = jnp.sum(weights[..., None] * jnp.swapaxes(value_all, 0, 1)[None], axis=2)
    return pooled / total


def fused_kernel(
    x_ref, w_ref, tok_ref, g_ref, u_ref, head_ref, q_ref, live_ref, tail_ref, kv_ref, gacc, uacc
):
    j = pl.program_id(0)

    @pl.when(j == 0)
    def _():
        kv_ref[...] = jnp.zeros_like(kv_ref)
        gacc[...] = jnp.zeros_like(gacc)
        uacc[...] = jnp.zeros_like(uacc)

    group, rows, _ = w_ref.shape
    acc = jnp.dot(x_ref[:, 0:rows], w_ref[0], preferred_element_type=jnp.float32)
    for i in range(1, group):
        acc += jnp.dot(
            x_ref[:, i * rows : (i + 1) * rows], w_ref[i], preferred_element_type=jnp.float32
        )
    kv_ref[...] += acc

    t = tok_ref[...]
    k = g_ref.shape[0] * g_ref.shape[1]
    gacc[...] += jnp.dot(t, g_ref[...].reshape(k, -1), preferred_element_type=jnp.float32)
    uacc[...] += jnp.dot(t, u_ref[...].reshape(k, -1), preferred_element_type=jnp.float32)

    @pl.when(j == pl.num_programs(0) - 1)
    def _():
        g = gacc[...]
        act = g / (1.0 + jnp.exp(-g))
        col = jnp.sum(act * uacc[...] * head_ref[...], axis=1, keepdims=True)
        wide = jnp.broadcast_to(col, (col.shape[0], 128))
        row = jnp.transpose(wide)[0:1, :]
        width = tail_ref.shape[1]
        score_rows = row.shape[1] // width
        for r in range(score_rows):
            tail_ref[r : r + 1, :] = row[:, r * width : (r + 1) * width]
        segs = q_ref.shape[0]
        kv = kv_ref[...]
        keys = kv[:, 0:width].reshape(segs, -1, width)
        values = kv[:, width:].reshape(segs, -1, width)
        prod = keys * q_ref[...]
        for h in range(width // HD):
            lanes = slice(h * HD, (h + 1) * HD)
            sc = jnp.sum(prod[:, :, lanes], axis=2, keepdims=True) / math.sqrt(HD)
            sc = sc - jnp.max(sc, axis=1, keepdims=True)
            wt = jnp.exp(sc)
            wt = wt / jnp.sum(wt, axis=1, keepdims=True)
            r0 = score_rows
            tail_ref[r0 : r0 + segs, lanes] = jnp.sum(wt * keys[:, :, lanes], axis=1)
            r0 = score_rows + segs
            tail_ref[r0 : r0 + segs, lanes] = jnp.sum(wt * values[:, :, lanes], axis=1)
        tail_ref[score_rows + 2 * segs :, :] = live_ref[...]


def project_all(normed, tokens, gathered, head, queries, live_row, kv_rows, d_rows, steps):
    n_dev, _, cols = gathered.shape
    n_norm = normed.shape[0]
    n_tok = tokens.shape[0]
    segs = queries.shape[0]
    width = queries.shape[2]
    tail_rows = n_tok // width + 2 * segs + 1
    group = n_dev // steps
    gate_blk = kv_rows // d_rows
    return pl.pallas_call(
        fused_kernel,
        grid=(steps,),
        in_specs=[
            pl.BlockSpec((n_norm, group * kv_rows), lambda j: (0, j)),
            pl.BlockSpec((group, kv_rows, cols), lambda j: (j, 0, 0)),
            pl.BlockSpec((n_tok, group * d_rows), lambda j: (0, j)),
            pl.BlockSpec((group, d_rows, cols), lambda j: (j, gate_blk, 0)),
            pl.BlockSpec((group, d_rows, cols), lambda j: (j, gate_blk + 1, 0)),
            pl.BlockSpec((1, cols), lambda j: (0, 0)),
            pl.BlockSpec(queries.shape, lambda j: (0, 0, 0)),
            pl.BlockSpec(live_row.shape, lambda j: (0, 0)),
        ],
        out_specs=pl.BlockSpec((tail_rows, width), lambda j: (0, 0)),
        out_shape=jax.ShapeDtypeStruct((tail_rows, width), jnp.float32),
        scratch_shapes=[
            pltpu.VMEM((n_norm, cols), jnp.float32),
            pltpu.VMEM((n_tok, cols), jnp.float32),
            pltpu.VMEM((n_tok, cols), jnp.float32),
        ],
    )(normed, gathered, tokens, gathered, gathered, head.reshape(1, cols), queries, live_row)


def local(
    draft_tokens,
    draft_gate,
    draft_up,
    draft_head,
    verifier_rows,
    norm_gain,
    key_weight,
    value_weight,
    pool_query,
    flags,
    owner,
):
    seg_count = flags.shape[0]
    n_seq = lax.axis_size("seq")
    n_fsdp = lax.axis_size("fsdp")
    d_rows, d_cols = draft_gate.shape
    v_rows = key_weight.shape[0]
    kv_cols = key_weight.shape[1]
    kv_block = jnp.concatenate([key_weight, value_weight], axis=1)
    kv_block = kv_block.reshape(-1, d_cols)
    block = jnp.concatenate([kv_block, draft_gate, draft_up], axis=0)
    gathered = lax.all_gather(block, "fsdp", axis=0, tiled=False)
    kv_rows = kv_block.shape[0]

    normed = normalize_rows(verifier_rows, norm_gain)
    lane_pick = (
        owner[:, None] == jnp.arange(pool_query.shape[0], dtype=jnp.int32)[None, :]
    ).astype(jnp.float32)
    queries = jnp.einsum("sc,chd->shd", lane_pick, pool_query, precision=lax.Precision.HIGHEST)
    width = KVH * HD
    live_row = jnp.zeros((1, width), jnp.float32).at[0, :seg_count].set(flags.astype(jnp.float32))
    tail = project_all(
        normed,
        draft_tokens,
        gathered,
        draft_head,
        queries.reshape(seg_count, 1, width),
        live_row,
        kv_rows,
        d_rows,
        4,
    )
    score_rows = draft_tokens.shape[0] // width
    summary_key = tail[score_rows : score_rows + seg_count].reshape(seg_count, KVH, HD)
    tails = [tail] + [
        lax.ppermute(tail, "seq", [(i, (i + k) % n_seq) for i in range(n_seq)])
        for k in range(1, n_seq)
    ]
    own = lax.axis_index("seq")
    own_tokens = seg_count * SEGL
    token_scores = sum(
        lax.dynamic_slice_in_dim(t[:score_rows].reshape(-1), own * own_tokens, own_tokens)
        for t in tails
    )
    draft_score = jnp.mean(token_scores.reshape(seg_count, SEGL), axis=1)
    query_keys = summary_key[:, :, None, :]
    scores, lives = [], []
    for t in tails:
        keys = t[score_rows : score_rows + seg_count].reshape(seg_count, KVH, HD)
        live = t[score_rows + 2 * seg_count, :seg_count] > 0.5
        sc = jnp.sum(query_keys * jnp.swapaxes(keys, 0, 1)[None], axis=-1) / math.sqrt(HD)
        scores.append(jnp.where(live[None, None, :], sc, -1e30))
        lives.append(live)
    highest = scores[0].max(axis=2, keepdims=True)
    for sc in scores[1:]:
        highest = jnp.maximum(highest, sc.max(axis=2, keepdims=True))
    total = 0.0
    pooled = 0.0
    for t, sc, live in zip(tails, scores, lives):
        values = t[score_rows + seg_count : score_rows + 2 * seg_count].reshape(seg_count, KVH, HD)
        wt = jnp.where(live[None, None, :], jnp.exp(sc - highest), 0.0)
        total = total + jnp.sum(wt, axis=2, keepdims=True)
        pooled = pooled + jnp.sum(wt[..., None] * jnp.swapaxes(values, 0, 1)[None], axis=2)
    pooled = pooled / total
    own_pooled = pooled.reshape(seg_count, KVH * HD)
    verdict = jnp.where(
        flags[:, None] == 1, jax.nn.sigmoid(draft_score)[:, None] * own_pooled, 0.0
    ).astype(jnp.bfloat16)
    return (draft_score, verdict)


def solution(mesh):
    return jax.shard_map(
        local,
        mesh=mesh,
        in_specs=(
            P("fsdp", None),
            P("fsdp", "seq"),
            P("fsdp", "seq"),
            P("seq"),
            P(("fsdp", "seq"), None),
            P(),
            P("fsdp", None),
            P("fsdp", None),
            P(),
            P(("fsdp", "seq")),
            P(("fsdp", "seq")),
        ),
        out_specs=(P(("fsdp", "seq")), P(("fsdp", "seq"), None)),
        check_vma=False,
    )
```

```python
import math

import jax
import jax.numpy as jnp
from jax import lax
from jax.experimental import pallas as pl
from jax.experimental.pallas import tpu as pltpu
from jax.sharding import PartitionSpec as P

KVH = 4
HD = 128
SEGL = 32


eps = 1e-05


def normalize_rows(rows, norm_gain):
    values = rows.astype(jnp.float32)
    scale = lax.rsqrt(jnp.mean(values * values, axis=-1, keepdims=True) + eps)
    return (values * scale * norm_gain).astype(jnp.bfloat16)


def segment_pool(seg_keys, seg_values, queries, head_size):
    scores = jnp.sum(seg_keys * queries[:, None], axis=-1) / math.sqrt(head_size)
    scores = scores - jnp.max(scores, axis=1, keepdims=True)
    weights = jnp.exp(scores)
    weights = weights / jnp.sum(weights, axis=1, keepdims=True)
    summary_key = jnp.sum(weights[..., None] * seg_keys, axis=1)
    summary_value = jnp.sum(weights[..., None] * seg_values, axis=1)
    return (summary_key, summary_value)


def cross_pool(query_keys, key_all, value_all, live_all, head_size):
    scores = jnp.sum(query_keys[:, :, None, :] * jnp.swapaxes(key_all, 0, 1)[None], axis=-1)
    scores = scores / math.sqrt(head_size)
    scores = jnp.where(live_all[None, None, :], scores, -1e30)
    highest = jnp.max(scores, axis=2, keepdims=True)
    weights = jnp.where(live_all[None, None, :], jnp.exp(scores - highest), 0.0)
    total = jnp.sum(weights, axis=2, keepdims=True)
    pooled = jnp.sum(weights[..., None] * jnp.swapaxes(value_all, 0, 1)[None], axis=2)
    return pooled / total


def fused_kernel(
    x_ref, w_ref, tok_ref, g_ref, u_ref, head_ref, q_ref, live_ref, tail_ref, kv_ref, gacc, uacc
):
    j = pl.program_id(0)

    @pl.when(j == 0)
    def _():
        kv_ref[...] = jnp.zeros_like(kv_ref)
        gacc[...] = jnp.zeros_like(gacc)
        uacc[...] = jnp.zeros_like(uacc)

    group, rows, _ = w_ref.shape
    acc = jnp.dot(x_ref[:, 0:rows], w_ref[0], preferred_element_type=jnp.float32)
    for i in range(1, group):
        acc += jnp.dot(
            x_ref[:, i * rows : (i + 1) * rows], w_ref[i], preferred_element_type=jnp.float32
        )
    kv_ref[...] += acc

    t = tok_ref[...]
    k = g_ref.shape[0] * g_ref.shape[1]
    gacc[...] += jnp.dot(t, g_ref[...].reshape(k, -1), preferred_element_type=jnp.float32)
    uacc[...] += jnp.dot(t, u_ref[...].reshape(k, -1), preferred_element_type=jnp.float32)

    @pl.when(j == pl.num_programs(0) - 1)
    def _():
        g = gacc[...]
        act = g / (1.0 + jnp.exp(-g))
        col = jnp.sum(act * uacc[...] * head_ref[...], axis=1, keepdims=True)
        wide = jnp.broadcast_to(col, (col.shape[0], 128))
        row = jnp.transpose(wide)[0:1, :]
        width = tail_ref.shape[1]
        score_rows = row.shape[1] // width
        for r in range(score_rows):
            tail_ref[r : r + 1, :] = row[:, r * width : (r + 1) * width]
        segs = q_ref.shape[0]
        kv = kv_ref[...]
        keys = kv[:, 0:width].reshape(segs, -1, width)
        values = kv[:, width:].reshape(segs, -1, width)
        prod = keys * q_ref[...]
        for h in range(width // HD):
            lanes = slice(h * HD, (h + 1) * HD)
            sc = jnp.sum(prod[:, :, lanes], axis=2, keepdims=True) / math.sqrt(HD)
            sc = sc - jnp.max(sc, axis=1, keepdims=True)
            wt = jnp.exp(sc)
            wt = wt / jnp.sum(wt, axis=1, keepdims=True)
            r0 = score_rows
            tail_ref[r0 : r0 + segs, lanes] = jnp.sum(wt * keys[:, :, lanes], axis=1)
            r0 = score_rows + segs
            tail_ref[r0 : r0 + segs, lanes] = jnp.sum(wt * values[:, :, lanes], axis=1)
        tail_ref[score_rows + 2 * segs :, :] = live_ref[...]


def project_all(normed, tokens, gathered, head, queries, live_row, kv_rows, d_rows, steps):
    n_dev, _, cols = gathered.shape
    n_norm = normed.shape[0]
    n_tok = tokens.shape[0]
    segs = queries.shape[0]
    width = queries.shape[2]
    tail_rows = n_tok // width + 2 * segs + 1
    group = n_dev // steps
    gate_blk = kv_rows // d_rows
    return pl.pallas_call(
        fused_kernel,
        grid=(steps,),
        in_specs=[
            pl.BlockSpec((n_norm, group * kv_rows), lambda j: (0, j)),
            pl.BlockSpec((group, kv_rows, cols), lambda j: (j, 0, 0)),
            pl.BlockSpec((n_tok, group * d_rows), lambda j: (0, j)),
            pl.BlockSpec((group, d_rows, cols), lambda j: (j, gate_blk, 0)),
            pl.BlockSpec((group, d_rows, cols), lambda j: (j, gate_blk + 1, 0)),
            pl.BlockSpec((1, cols), lambda j: (0, 0)),
            pl.BlockSpec(queries.shape, lambda j: (0, 0, 0)),
            pl.BlockSpec(live_row.shape, lambda j: (0, 0)),
        ],
        out_specs=pl.BlockSpec((tail_rows, width), lambda j: (0, 0)),
        out_shape=jax.ShapeDtypeStruct((tail_rows, width), jnp.float32),
        scratch_shapes=[
            pltpu.VMEM((n_norm, cols), jnp.float32),
            pltpu.VMEM((n_tok, cols), jnp.float32),
            pltpu.VMEM((n_tok, cols), jnp.float32),
        ],
    )(normed, gathered, tokens, gathered, gathered, head.reshape(1, cols), queries, live_row)


def pack_kernel(k_ref, v_ref, g_ref, u_ref, out_ref):
    rows, half = k_ref.shape
    d_rows = g_ref.shape[0]
    out_ref[0:rows, 0:half] = k_ref[...]
    out_ref[0:rows, half:] = v_ref[...]
    out_ref[rows : rows + d_rows, :] = g_ref[...]
    out_ref[rows + d_rows :, :] = u_ref[...]


def pack_block(key_weight, value_weight, draft_gate, draft_up):
    rows = key_weight.shape[0]
    d_rows, cols = draft_gate.shape
    return pl.pallas_call(
        pack_kernel,
        out_shape=jax.ShapeDtypeStruct((rows + 2 * d_rows, cols), key_weight.dtype),
    )(key_weight, value_weight, draft_gate, draft_up)


def local(
    draft_tokens,
    draft_gate,
    draft_up,
    draft_head,
    verifier_rows,
    norm_gain,
    key_weight,
    value_weight,
    pool_query,
    flags,
    owner,
):
    seg_count = flags.shape[0]
    n_seq = lax.axis_size("seq")
    n_fsdp = lax.axis_size("fsdp")
    d_rows, d_cols = draft_gate.shape
    v_rows = key_weight.shape[0]
    kv_cols = key_weight.shape[1]
    block = pack_block(key_weight, value_weight, draft_gate, draft_up)
    gathered = lax.all_gather(block, "fsdp", axis=0, tiled=False)
    kv_rows = key_weight.shape[0]

    normed = normalize_rows(verifier_rows, norm_gain)
    lane_pick = (
        owner[:, None] == jnp.arange(pool_query.shape[0], dtype=jnp.int32)[None, :]
    ).astype(jnp.float32)
    queries = jnp.einsum("sc,chd->shd", lane_pick, pool_query, precision=lax.Precision.HIGHEST)
    width = KVH * HD
    live_row = jnp.zeros((1, width), jnp.float32).at[0, :seg_count].set(flags.astype(jnp.float32))
    tail = project_all(
        normed,
        draft_tokens,
        gathered,
        draft_head,
        queries.reshape(seg_count, 1, width),
        live_row,
        kv_rows,
        d_rows,
        4,
    )
    score_rows = draft_tokens.shape[0] // width
    summary_key = tail[score_rows : score_rows + seg_count].reshape(seg_count, KVH, HD)
    tail_all = jnp.stack(
        [tail]
        + [
            lax.ppermute(tail, "seq", [(i, (i + k) % n_seq) for i in range(n_seq)])
            for k in range(1, n_seq)
        ]
    )
    scores_all = tail_all[:, :score_rows].reshape(n_seq, -1)
    summary_all = tail_all[:, score_rows:]
    own = lax.axis_index("seq")
    own_tokens = seg_count * SEGL
    token_scores = jnp.sum(
        lax.dynamic_slice_in_dim(scores_all, own * own_tokens, own_tokens, axis=1), axis=0
    )
    draft_score = jnp.mean(token_scores.reshape(seg_count, SEGL), axis=1)
    key_all = summary_all[:, :seg_count].reshape(-1, KVH, HD)
    value_all = summary_all[:, seg_count : 2 * seg_count].reshape(-1, KVH, HD)
    live_all = summary_all[:, 2 * seg_count, :seg_count].reshape(-1)
    pooled = cross_pool(
        summary_key,
        key_all,
        value_all,
        live_all > 0.5,
        HD,
    )
    own_pooled = pooled.reshape(seg_count, KVH * HD)
    verdict = jnp.where(
        flags[:, None] == 1, jax.nn.sigmoid(draft_score)[:, None] * own_pooled, 0.0
    ).astype(jnp.bfloat16)
    return (draft_score, verdict)


def solution(mesh):
    return jax.shard_map(
        local,
        mesh=mesh,
        in_specs=(
            P("fsdp", None),
            P("fsdp", "seq"),
            P("fsdp", "seq"),
            P("seq"),
            P(("fsdp", "seq"), None),
            P(),
            P("fsdp", None),
            P("fsdp", None),
            P(),
            P(("fsdp", "seq")),
            P(("fsdp", "seq")),
        ),
        out_specs=(P(("fsdp", "seq")), P(("fsdp", "seq"), None)),
        check_vma=False,
    )
```

```python
import math

import jax
import jax.numpy as jnp
from jax import lax
from jax.experimental import pallas as pl
from jax.experimental.pallas import tpu as pltpu
from jax.sharding import PartitionSpec as P

KVH = 4
HD = 128
SEGL = 32


eps = 1e-05


def normalize_rows(rows, norm_gain):
    values = rows.astype(jnp.float32)
    scale = lax.rsqrt(jnp.mean(values * values, axis=-1, keepdims=True) + eps)
    return (values * scale * norm_gain).astype(jnp.bfloat16)


def segment_pool(seg_keys, seg_values, queries, head_size):
    scores = jnp.sum(seg_keys * queries[:, None], axis=-1) / math.sqrt(head_size)
    scores = scores - jnp.max(scores, axis=1, keepdims=True)
    weights = jnp.exp(scores)
    weights = weights / jnp.sum(weights, axis=1, keepdims=True)
    summary_key = jnp.sum(weights[..., None] * seg_keys, axis=1)
    summary_value = jnp.sum(weights[..., None] * seg_values, axis=1)
    return (summary_key, summary_value)


def cross_pool(query_keys, key_all, value_all, live_all, head_size):
    scores = jnp.sum(query_keys[:, :, None, :] * jnp.swapaxes(key_all, 0, 1)[None], axis=-1)
    scores = scores / math.sqrt(head_size)
    scores = jnp.where(live_all[None, None, :], scores, -1e30)
    highest = jnp.max(scores, axis=2, keepdims=True)
    weights = jnp.where(live_all[None, None, :], jnp.exp(scores - highest), 0.0)
    total = jnp.sum(weights, axis=2, keepdims=True)
    pooled = jnp.sum(weights[..., None] * jnp.swapaxes(value_all, 0, 1)[None], axis=2)
    return pooled / total


def fused_kernel(x_ref, w_ref, tok_ref, g_ref, u_ref, head_ref, kv_ref, score_ref, gacc, uacc):
    j = pl.program_id(0)

    @pl.when(j == 0)
    def _():
        kv_ref[...] = jnp.zeros_like(kv_ref)
        gacc[...] = jnp.zeros_like(gacc)
        uacc[...] = jnp.zeros_like(uacc)

    group, rows, _ = w_ref.shape
    acc = jnp.dot(x_ref[:, 0:rows], w_ref[0], preferred_element_type=jnp.float32)
    for i in range(1, group):
        acc += jnp.dot(
            x_ref[:, i * rows : (i + 1) * rows], w_ref[i], preferred_element_type=jnp.float32
        )
    kv_ref[...] += acc

    t = tok_ref[...]
    k = g_ref.shape[0] * g_ref.shape[1]
    gacc[...] += jnp.dot(t, g_ref[...].reshape(k, -1), preferred_element_type=jnp.float32)
    uacc[...] += jnp.dot(t, u_ref[...].reshape(k, -1), preferred_element_type=jnp.float32)

    @pl.when(j == pl.num_programs(0) - 1)
    def _():
        g = gacc[...]
        act = g * (0.5 + 0.5 * jnp.tanh(0.5 * g))
        col = jnp.sum(act * uacc[...] * head_ref[...], axis=1, keepdims=True)
        wide = jnp.broadcast_to(col, (col.shape[0], 128))
        score_ref[...] = jnp.transpose(wide)[0 : score_ref.shape[0], :]


def project_all(normed, tokens, gathered, head, kv_rows, d_rows, steps):
    n_dev, _, cols = gathered.shape
    n_norm = normed.shape[0]
    n_tok = tokens.shape[0]
    group = n_dev // steps
    gate_blk = kv_rows // d_rows
    seg_kv, scores = pl.pallas_call(
        fused_kernel,
        grid=(steps,),
        in_specs=[
            pl.BlockSpec((n_norm, group * kv_rows), lambda j: (0, j)),
            pl.BlockSpec((group, kv_rows, cols), lambda j: (j, 0, 0)),
            pl.BlockSpec((n_tok, group * d_rows), lambda j: (0, j)),
            pl.BlockSpec((group, d_rows, cols), lambda j: (j, gate_blk, 0)),
            pl.BlockSpec((group, d_rows, cols), lambda j: (j, gate_blk + 1, 0)),
            pl.BlockSpec((1, cols), lambda j: (0, 0)),
        ],
        out_specs=[
            pl.BlockSpec((n_norm, cols), lambda j: (0, 0)),
            pl.BlockSpec((8, n_tok), lambda j: (0, 0)),
        ],
        out_shape=[
            jax.ShapeDtypeStruct((n_norm, cols), jnp.float32),
            jax.ShapeDtypeStruct((8, n_tok), jnp.float32),
        ],
        scratch_shapes=[
            pltpu.VMEM((n_tok, cols), jnp.float32),
            pltpu.VMEM((n_tok, cols), jnp.float32),
        ],
    )(normed, gathered, tokens, gathered, gathered, head.reshape(1, cols))
    return seg_kv, scores[0]


def local(
    draft_tokens,
    draft_gate,
    draft_up,
    draft_head,
    verifier_rows,
    norm_gain,
    key_weight,
    value_weight,
    pool_query,
    flags,
    owner,
):
    seg_count = flags.shape[0]
    n_seq = lax.axis_size("seq")
    n_fsdp = lax.axis_size("fsdp")
    d_rows, d_cols = draft_gate.shape
    v_rows = key_weight.shape[0]
    kv_cols = key_weight.shape[1]
    kv_block = jnp.concatenate([key_weight, value_weight], axis=1)
    kv_block = kv_block.reshape(-1, d_cols)
    block = jnp.concatenate([kv_block, draft_gate, draft_up], axis=0)
    gathered = lax.all_gather(block, "fsdp", axis=0, tiled=False)
    kv_rows = kv_block.shape[0]

    normed = normalize_rows(verifier_rows, norm_gain)
    seg_kv, partial_scores = project_all(
        normed, draft_tokens, gathered, draft_head, kv_rows, d_rows, 4
    )
    seg_keys = seg_kv[:, :kv_cols]
    seg_values = seg_kv[:, kv_cols:]
    lane_pick = (
        owner[:, None] == jnp.arange(pool_query.shape[0], dtype=jnp.int32)[None, :]
    ).astype(jnp.float32)
    queries = jnp.einsum("sc,chd->shd", lane_pick, pool_query, precision=lax.Precision.HIGHEST)
    summary_key, summary_value = segment_pool(
        seg_keys.reshape(seg_count, SEGL, KVH, HD),
        seg_values.reshape(seg_count, SEGL, KVH, HD),
        queries,
        HD,
    )
    width = KVH * HD
    live_row = jnp.zeros((1, width), jnp.float32).at[0, :seg_count].set(flags.astype(jnp.float32))
    tail = jnp.concatenate(
        [
            partial_scores.reshape(-1, width),
            summary_key.reshape(seg_count, width),
            summary_value.reshape(seg_count, width),
            live_row,
        ],
        axis=0,
    )
    tail_all = jnp.stack(
        [tail]
        + [
            lax.ppermute(tail, "seq", [(i, (i + k) % n_seq) for i in range(n_seq)])
            for k in range(1, n_seq)
        ]
    )
    score_rows = partial_scores.shape[0] // width
    scores_all = tail_all[:, :score_rows].reshape(n_seq, -1)
    summary_all = tail_all[:, score_rows:]
    own = lax.axis_index("seq")
    own_tokens = seg_count * SEGL
    token_scores = jnp.sum(
        lax.dynamic_slice_in_dim(scores_all, own * own_tokens, own_tokens, axis=1), axis=0
    )
    draft_score = jnp.mean(token_scores.reshape(seg_count, SEGL), axis=1)
    key_all = summary_all[:, :seg_count].reshape(-1, KVH, HD)
    value_all = summary_all[:, seg_count : 2 * seg_count].reshape(-1, KVH, HD)
    live_all = summary_all[:, 2 * seg_count, :seg_count].reshape(-1)
    pooled = cross_pool(
        summary_key,
        key_all,
        value_all,
        live_all > 0.5,
        HD,
    )
    own_pooled = pooled.reshape(seg_count, KVH * HD)
    verdict = jnp.where(
        flags[:, None] == 1, jax.nn.sigmoid(draft_score)[:, None] * own_pooled, 0.0
    ).astype(jnp.bfloat16)
    return (draft_score, verdict)


def solution(mesh):
    return jax.shard_map(
        local,
        mesh=mesh,
        in_specs=(
            P("fsdp", None),
            P("fsdp", "seq"),
            P("fsdp", "seq"),
            P("seq"),
            P(("fsdp", "seq"), None),
            P(),
            P("fsdp", None),
            P("fsdp", None),
            P(),
            P(("fsdp", "seq")),
            P(("fsdp", "seq")),
        ),
        out_specs=(P(("fsdp", "seq")), P(("fsdp", "seq"), None)),
        check_vma=False,
    )
```

```python
import math

import jax
import jax.numpy as jnp
from jax import lax
from jax.experimental import pallas as pl
from jax.experimental.pallas import tpu as pltpu
from jax.sharding import PartitionSpec as P

KVH = 4
HD = 128
SEGL = 32


eps = 1e-05


def normalize_rows(rows, norm_gain):
    values = rows.astype(jnp.float32)
    scale = lax.rsqrt(jnp.mean(values * values, axis=-1, keepdims=True) + eps)
    return (values * scale * norm_gain).astype(jnp.bfloat16)


def segment_pool(seg_keys, seg_values, queries, head_size):
    scores = jnp.sum(seg_keys * queries[:, None], axis=-1) / math.sqrt(head_size)
    scores = scores - jnp.max(scores, axis=1, keepdims=True)
    weights = jnp.exp(scores)
    weights = weights / jnp.sum(weights, axis=1, keepdims=True)
    summary_key = jnp.sum(weights[..., None] * seg_keys, axis=1)
    summary_value = jnp.sum(weights[..., None] * seg_values, axis=1)
    return (summary_key, summary_value)


def cross_pool(query_keys, key_all, value_all, live_all, head_size):
    scores = jnp.sum(query_keys[:, :, None, :] * jnp.swapaxes(key_all, 0, 1)[None], axis=-1)
    scores = scores / math.sqrt(head_size)
    scores = jnp.where(live_all[None, None, :], scores, -1e30)
    highest = jnp.max(scores, axis=2, keepdims=True)
    weights = jnp.where(live_all[None, None, :], jnp.exp(scores - highest), 0.0)
    total = jnp.sum(weights, axis=2, keepdims=True)
    pooled = jnp.sum(weights[..., None] * jnp.swapaxes(value_all, 0, 1)[None], axis=2)
    return pooled / total


def fused_kernel(x_ref, w_ref, tok_ref, g_ref, u_ref, head_ref, kv_ref, score_ref, gacc, uacc):
    j = pl.program_id(0)

    @pl.when(j == 0)
    def _():
        kv_ref[...] = jnp.zeros_like(kv_ref)
        gacc[...] = jnp.zeros_like(gacc)
        uacc[...] = jnp.zeros_like(uacc)

    group, rows, _ = w_ref.shape
    acc = jnp.dot(x_ref[:, 0:rows], w_ref[0], preferred_element_type=jnp.float32)
    for i in range(1, group):
        acc += jnp.dot(
            x_ref[:, i * rows : (i + 1) * rows], w_ref[i], preferred_element_type=jnp.float32
        )
    kv_ref[...] += acc

    sub = g_ref.shape[0] // 2
    k = sub * g_ref.shape[1]
    h = j % 2
    t = tok_ref[:, pl.ds(pl.multiple_of(h * k, k), k)]
    g_w = g_ref[pl.ds(h * sub, sub)].reshape(k, -1)
    u_w = u_ref[pl.ds(h * sub, sub)].reshape(k, -1)
    gacc[...] += jnp.dot(t, g_w, preferred_element_type=jnp.float32)
    uacc[...] += jnp.dot(t, u_w, preferred_element_type=jnp.float32)

    @pl.when(j == pl.num_programs(0) - 1)
    def _():
        g = gacc[...]
        act = g / (1.0 + jnp.exp(-g))
        col = jnp.sum(act * uacc[...] * head_ref[...], axis=1, keepdims=True)
        wide = jnp.broadcast_to(col, (col.shape[0], 128))
        score_ref[...] = jnp.transpose(wide)[0 : score_ref.shape[0], :]


def project_all(normed, tokens, gathered, head, kv_rows, d_rows, steps):
    n_dev, _, cols = gathered.shape
    n_norm = normed.shape[0]
    n_tok = tokens.shape[0]
    group = n_dev // steps
    d_group = 2 * group
    gate_blk = kv_rows // d_rows
    seg_kv, scores = pl.pallas_call(
        fused_kernel,
        grid=(steps,),
        in_specs=[
            pl.BlockSpec((n_norm, group * kv_rows), lambda j: (0, j)),
            pl.BlockSpec((group, kv_rows, cols), lambda j: (j, 0, 0)),
            pl.BlockSpec((n_tok, d_group * d_rows), lambda j: (0, j // 2)),
            pl.BlockSpec((d_group, d_rows, cols), lambda j: (j // 2, gate_blk, 0)),
            pl.BlockSpec((d_group, d_rows, cols), lambda j: (j // 2, gate_blk + 1, 0)),
            pl.BlockSpec((1, cols), lambda j: (0, 0)),
        ],
        out_specs=[
            pl.BlockSpec((n_norm, cols), lambda j: (0, 0)),
            pl.BlockSpec((8, n_tok), lambda j: (0, 0)),
        ],
        out_shape=[
            jax.ShapeDtypeStruct((n_norm, cols), jnp.float32),
            jax.ShapeDtypeStruct((8, n_tok), jnp.float32),
        ],
        scratch_shapes=[
            pltpu.VMEM((n_tok, cols), jnp.float32),
            pltpu.VMEM((n_tok, cols), jnp.float32),
        ],
    )(normed, gathered, tokens, gathered, gathered, head.reshape(1, cols))
    return seg_kv, scores[0]


def local(
    draft_tokens,
    draft_gate,
    draft_up,
    draft_head,
    verifier_rows,
    norm_gain,
    key_weight,
    value_weight,
    pool_query,
    flags,
    owner,
):
    seg_count = flags.shape[0]
    n_seq = lax.axis_size("seq")
    n_fsdp = lax.axis_size("fsdp")
    d_rows, d_cols = draft_gate.shape
    v_rows = key_weight.shape[0]
    kv_cols = key_weight.shape[1]
    kv_block = jnp.concatenate([key_weight, value_weight], axis=1)
    kv_block = kv_block.reshape(-1, d_cols)
    block = jnp.concatenate([kv_block, draft_gate, draft_up], axis=0)
    gathered = lax.all_gather(block, "fsdp", axis=0, tiled=False)
    kv_rows = kv_block.shape[0]

    normed = normalize_rows(verifier_rows, norm_gain)
    seg_kv, partial_scores = project_all(
        normed, draft_tokens, gathered, draft_head, kv_rows, d_rows, 8
    )
    seg_keys = seg_kv[:, :kv_cols]
    seg_values = seg_kv[:, kv_cols:]
    lane_pick = (
        owner[:, None] == jnp.arange(pool_query.shape[0], dtype=jnp.int32)[None, :]
    ).astype(jnp.float32)
    queries = jnp.einsum("sc,chd->shd", lane_pick, pool_query, precision=lax.Precision.HIGHEST)
    summary_key, summary_value = segment_pool(
        seg_keys.reshape(seg_count, SEGL, KVH, HD),
        seg_values.reshape(seg_count, SEGL, KVH, HD),
        queries,
        HD,
    )
    width = KVH * HD
    live_row = jnp.zeros((1, width), jnp.float32).at[0, :seg_count].set(flags.astype(jnp.float32))
    tail = jnp.concatenate(
        [
            partial_scores.reshape(-1, width),
            summary_key.reshape(seg_count, width),
            summary_value.reshape(seg_count, width),
            live_row,
        ],
        axis=0,
    )
    tail_all = jnp.stack(
        [tail]
        + [
            lax.ppermute(tail, "seq", [(i, (i + k) % n_seq) for i in range(n_seq)])
            for k in range(1, n_seq)
        ]
    )
    score_rows = partial_scores.shape[0] // width
    scores_all = tail_all[:, :score_rows].reshape(n_seq, -1)
    summary_all = tail_all[:, score_rows:]
    own = lax.axis_index("seq")
    own_tokens = seg_count * SEGL
    token_scores = jnp.sum(
        lax.dynamic_slice_in_dim(scores_all, own * own_tokens, own_tokens, axis=1), axis=0
    )
    draft_score = jnp.mean(token_scores.reshape(seg_count, SEGL), axis=1)
    key_all = summary_all[:, :seg_count].reshape(-1, KVH, HD)
    value_all = summary_all[:, seg_count : 2 * seg_count].reshape(-1, KVH, HD)
    live_all = summary_all[:, 2 * seg_count, :seg_count].reshape(-1)
    pooled = cross_pool(
        summary_key,
        key_all,
        value_all,
        live_all > 0.5,
        HD,
    )
    own_pooled = pooled.reshape(seg_count, KVH * HD)
    verdict = jnp.where(
        flags[:, None] == 1, jax.nn.sigmoid(draft_score)[:, None] * own_pooled, 0.0
    ).astype(jnp.bfloat16)
    return (draft_score, verdict)


def solution(mesh):
    return jax.shard_map(
        local,
        mesh=mesh,
        in_specs=(
            P("fsdp", None),
            P("fsdp", "seq"),
            P("fsdp", "seq"),
            P("seq"),
            P(("fsdp", "seq"), None),
            P(),
            P("fsdp", None),
            P("fsdp", None),
            P(),
            P(("fsdp", "seq")),
            P(("fsdp", "seq")),
        ),
        out_specs=(P(("fsdp", "seq")), P(("fsdp", "seq"), None)),
        check_vma=False,
    )
```

```python
import math

import jax
import jax.numpy as jnp
from jax import lax
from jax.experimental import pallas as pl
from jax.experimental.pallas import tpu as pltpu
from jax.sharding import PartitionSpec as P

KVH = 4
HD = 128
SEGL = 32


eps = 1e-05


def normalize_rows(rows, norm_gain):
    values = rows.astype(jnp.float32)
    scale = lax.rsqrt(jnp.mean(values * values, axis=-1, keepdims=True) + eps)
    return (values * scale * norm_gain).astype(jnp.bfloat16)


def segment_pool(seg_keys, seg_values, queries, head_size):
    scores = jnp.sum(seg_keys * queries[:, None], axis=-1) / math.sqrt(head_size)
    scores = scores - jnp.max(scores, axis=1, keepdims=True)
    weights = jnp.exp(scores)
    weights = weights / jnp.sum(weights, axis=1, keepdims=True)
    summary_key = jnp.sum(weights[..., None] * seg_keys, axis=1)
    summary_value = jnp.sum(weights[..., None] * seg_values, axis=1)
    return (summary_key, summary_value)


def cross_pool(query_keys, key_all, value_all, live_all, head_size):
    scores = jnp.sum(query_keys[:, :, None, :] * jnp.swapaxes(key_all, 0, 1)[None], axis=-1)
    scores = scores / math.sqrt(head_size)
    scores = jnp.where(live_all[None, None, :], scores, -1e30)
    highest = jnp.max(scores, axis=2, keepdims=True)
    weights = jnp.where(live_all[None, None, :], jnp.exp(scores - highest), 0.0)
    total = jnp.sum(weights, axis=2, keepdims=True)
    pooled = jnp.sum(weights[..., None] * jnp.swapaxes(value_all, 0, 1)[None], axis=2)
    return pooled / total


def fused_kernel(x_ref, w_ref, tok_ref, g_ref, u_ref, head_ref, kv_ref, score_ref, gacc, uacc):
    j = pl.program_id(0)

    @pl.when(j == 0)
    def _():
        kv_ref[...] = jnp.zeros_like(kv_ref)
        gacc[...] = jnp.zeros_like(gacc)
        uacc[...] = jnp.zeros_like(uacc)

    group, rows, _ = w_ref.shape
    acc = jnp.dot(x_ref[:, 0:rows], w_ref[0], preferred_element_type=jnp.float32)
    for i in range(1, group):
        acc += jnp.dot(
            x_ref[:, i * rows : (i + 1) * rows], w_ref[i], preferred_element_type=jnp.float32
        )
    kv_ref[...] += acc

    t = tok_ref[...]
    k = g_ref.shape[0] * g_ref.shape[1]
    gacc[...] += jnp.dot(t, g_ref[...].reshape(k, -1), preferred_element_type=jnp.float32)
    uacc[...] += jnp.dot(t, u_ref[...].reshape(k, -1), preferred_element_type=jnp.float32)

    @pl.when(j == pl.num_programs(0) - 1)
    def _():
        g = gacc[...]
        act = g / (1.0 + jnp.exp(-g))
        col = jnp.sum(act * uacc[...] * head_ref[...], axis=1, keepdims=True)
        wide = jnp.broadcast_to(col, (col.shape[0], 128))
        score_ref[...] = jnp.transpose(wide)[0 : score_ref.shape[0], :]


def project_all(normed, tokens, gathered, head, kv_rows, d_rows, steps):
    n_dev, _, cols = gathered.shape
    n_norm = normed.shape[0]
    n_tok = tokens.shape[0]
    group = n_dev // steps
    gate_blk = kv_rows // d_rows
    seg_kv, scores = pl.pallas_call(
        fused_kernel,
        grid=(steps,),
        in_specs=[
            pl.BlockSpec((n_norm, group * kv_rows), lambda j: (0, j)),
            pl.BlockSpec((group, kv_rows, cols), lambda j: (j, 0, 0)),
            pl.BlockSpec((n_tok, group * d_rows), lambda j: (0, j)),
            pl.BlockSpec((group, d_rows, cols), lambda j: (j, gate_blk, 0)),
            pl.BlockSpec((group, d_rows, cols), lambda j: (j, gate_blk + 1, 0)),
            pl.BlockSpec((1, cols), lambda j: (0, 0)),
        ],
        out_specs=[
            pl.BlockSpec((n_norm, cols), lambda j: (0, 0)),
            pl.BlockSpec((8, n_tok), lambda j: (0, 0)),
        ],
        out_shape=[
            jax.ShapeDtypeStruct((n_norm, cols), jnp.float32),
            jax.ShapeDtypeStruct((8, n_tok), jnp.float32),
        ],
        scratch_shapes=[
            pltpu.VMEM((n_tok, cols), jnp.float32),
            pltpu.VMEM((n_tok, cols), jnp.float32),
        ],
    )(normed, gathered, tokens, gathered, gathered, head.reshape(1, cols))
    return seg_kv, scores[0]


def local(
    draft_tokens,
    draft_gate,
    draft_up,
    draft_head,
    verifier_rows,
    norm_gain,
    key_weight,
    value_weight,
    pool_query,
    flags,
    owner,
):
    seg_count = flags.shape[0]
    n_seq = lax.axis_size("seq")
    n_fsdp = lax.axis_size("fsdp")
    d_rows, d_cols = draft_gate.shape
    v_rows = key_weight.shape[0]
    kv_cols = key_weight.shape[1]
    kv_block = jnp.concatenate([key_weight, value_weight], axis=1)
    kv_block = kv_block.reshape(-1, d_cols)
    block = jnp.concatenate([kv_block, draft_gate, draft_up], axis=0)
    gathered = lax.all_gather(block, "fsdp", axis=0, tiled=False)
    kv_rows = kv_block.shape[0]

    normed = normalize_rows(verifier_rows, norm_gain)
    seg_kv, partial_scores = project_all(
        normed, draft_tokens, gathered, draft_head, kv_rows, d_rows, 4
    )
    seg_keys = seg_kv[:, :kv_cols]
    seg_values = seg_kv[:, kv_cols:]
    lane_pick = (
        owner[:, None] == jnp.arange(pool_query.shape[0], dtype=jnp.int32)[None, :]
    ).astype(jnp.float32)
    queries = jnp.einsum("sc,chd->shd", lane_pick, pool_query, precision=lax.Precision.HIGHEST)
    summary_key, summary_value = segment_pool(
        seg_keys.reshape(seg_count, SEGL, KVH, HD),
        seg_values.reshape(seg_count, SEGL, KVH, HD),
        queries,
        HD,
    )
    width = KVH * HD
    live_row = jnp.zeros((1, width), jnp.float32).at[0, :seg_count].set(flags.astype(jnp.float32))
    tail = jnp.concatenate(
        [
            partial_scores.reshape(-1, width),
            summary_key.reshape(seg_count, width),
            summary_value.reshape(seg_count, width),
            live_row,
        ],
        axis=0,
    )
    tail_all = jnp.stack(
        [tail]
        + [
            lax.ppermute(tail, "seq", [(i, (i + k) % n_seq) for i in range(n_seq)])
            for k in sorted(range(1, n_seq), key=lambda k: min(k, n_seq - k))
        ]
    )
    score_rows = partial_scores.shape[0] // width
    scores_all = tail_all[:, :score_rows].reshape(n_seq, -1)
    summary_all = tail_all[:, score_rows:]
    own = lax.axis_index("seq")
    own_tokens = seg_count * SEGL
    token_scores = jnp.sum(
        lax.dynamic_slice_in_dim(scores_all, own * own_tokens, own_tokens, axis=1), axis=0
    )
    draft_score = jnp.mean(token_scores.reshape(seg_count, SEGL), axis=1)
    key_all = summary_all[:, :seg_count].reshape(-1, KVH, HD)
    value_all = summary_all[:, seg_count : 2 * seg_count].reshape(-1, KVH, HD)
    live_all = summary_all[:, 2 * seg_count, :seg_count].reshape(-1)
    pooled = cross_pool(
        summary_key,
        key_all,
        value_all,
        live_all > 0.5,
        HD,
    )
    own_pooled = pooled.reshape(seg_count, KVH * HD)
    verdict = jnp.where(
        flags[:, None] == 1, jax.nn.sigmoid(draft_score)[:, None] * own_pooled, 0.0
    ).astype(jnp.bfloat16)
    return (draft_score, verdict)


def solution(mesh):
    return jax.shard_map(
        local,
        mesh=mesh,
        in_specs=(
            P("fsdp", None),
            P("fsdp", "seq"),
            P("fsdp", "seq"),
            P("seq"),
            P(("fsdp", "seq"), None),
            P(),
            P("fsdp", None),
            P("fsdp", None),
            P(),
            P(("fsdp", "seq")),
            P(("fsdp", "seq")),
        ),
        out_specs=(P(("fsdp", "seq")), P(("fsdp", "seq"), None)),
        check_vma=False,
    )
```

```python
import math

import jax
import jax.numpy as jnp
from jax import lax
from jax.experimental import pallas as pl
from jax.experimental.pallas import tpu as pltpu
from jax.sharding import PartitionSpec as P

KVH = 4
HD = 128
SEGL = 32


eps = 1e-05


def normalize_rows(rows, norm_gain):
    values = rows.astype(jnp.float32)
    scale = lax.rsqrt(jnp.mean(values * values, axis=-1, keepdims=True) + eps)
    return (values * scale * norm_gain).astype(jnp.bfloat16)


def segment_pool(seg_keys, seg_values, queries, head_size):
    scores = jnp.sum(seg_keys * queries[:, None], axis=-1) / math.sqrt(head_size)
    scores = scores - jnp.max(scores, axis=1, keepdims=True)
    weights = jnp.exp(scores)
    weights = weights / jnp.sum(weights, axis=1, keepdims=True)
    summary_key = jnp.sum(weights[..., None] * seg_keys, axis=1)
    summary_value = jnp.sum(weights[..., None] * seg_values, axis=1)
    return (summary_key, summary_value)


def cross_pool(query_keys, key_all, value_all, live_all, head_size):
    scores = jnp.sum(query_keys[:, :, None, :] * jnp.swapaxes(key_all, 0, 1)[None], axis=-1)
    scores = scores / math.sqrt(head_size)
    scores = jnp.where(live_all[None, None, :], scores, -1e30)
    highest = jnp.max(scores, axis=2, keepdims=True)
    weights = jnp.where(live_all[None, None, :], jnp.exp(scores - highest), 0.0)
    total = jnp.sum(weights, axis=2, keepdims=True)
    pooled = jnp.sum(weights[..., None] * jnp.swapaxes(value_all, 0, 1)[None], axis=2)
    return pooled / total


def fused_kernel(x_ref, w_ref, tok_ref, g_ref, u_ref, head_ref, kv_ref, score_ref, gacc, uacc):
    j = pl.program_id(0)

    @pl.when(j == 0)
    def _():
        kv_ref[...] = jnp.zeros_like(kv_ref)
        gacc[...] = jnp.zeros_like(gacc)
        uacc[...] = jnp.zeros_like(uacc)

    group, rows, _ = w_ref.shape
    acc = jnp.dot(x_ref[:, 0:rows], w_ref[0], preferred_element_type=jnp.float32)
    for i in range(1, group):
        acc += jnp.dot(
            x_ref[:, i * rows : (i + 1) * rows], w_ref[i], preferred_element_type=jnp.float32
        )
    kv_ref[...] += acc

    t = tok_ref[...]
    k = g_ref.shape[0] * g_ref.shape[1]
    gacc[...] += jnp.dot(t, g_ref[...].reshape(k, -1), preferred_element_type=jnp.float32)
    uacc[...] += jnp.dot(t, u_ref[...].reshape(k, -1), preferred_element_type=jnp.float32)

    @pl.when(j == pl.num_programs(0) - 1)
    def _():
        g = gacc[...]
        act = g / (1.0 + jnp.exp(-g))
        col = jnp.sum(act * uacc[...] * head_ref[...], axis=1, keepdims=True)
        wide = jnp.broadcast_to(col, (col.shape[0], 128))
        row = jnp.transpose(wide)[0:1, :]
        width = score_ref.shape[1]
        for r in range(score_ref.shape[0]):
            score_ref[r : r + 1, :] = row[:, r * width : (r + 1) * width]


def project_all(normed, tokens, gathered, head, kv_rows, d_rows, steps):
    n_dev, _, cols = gathered.shape
    n_norm = normed.shape[0]
    n_tok = tokens.shape[0]
    group = n_dev // steps
    gate_blk = kv_rows // d_rows
    seg_kv, scores = pl.pallas_call(
        fused_kernel,
        grid=(steps,),
        in_specs=[
            pl.BlockSpec((n_norm, group * kv_rows), lambda j: (0, j)),
            pl.BlockSpec((group, kv_rows, cols), lambda j: (j, 0, 0)),
            pl.BlockSpec((n_tok, group * d_rows), lambda j: (0, j)),
            pl.BlockSpec((group, d_rows, cols), lambda j: (j, gate_blk, 0)),
            pl.BlockSpec((group, d_rows, cols), lambda j: (j, gate_blk + 1, 0)),
            pl.BlockSpec((1, cols), lambda j: (0, 0)),
        ],
        out_specs=[
            pl.BlockSpec((n_norm, cols), lambda j: (0, 0)),
            pl.BlockSpec((n_tok // (cols // 2), cols // 2), lambda j: (0, 0)),
        ],
        out_shape=[
            jax.ShapeDtypeStruct((n_norm, cols), jnp.float32),
            jax.ShapeDtypeStruct((n_tok // (cols // 2), cols // 2), jnp.float32),
        ],
        scratch_shapes=[
            pltpu.VMEM((n_tok, cols), jnp.float32),
            pltpu.VMEM((n_tok, cols), jnp.float32),
        ],
    )(normed, gathered, tokens, gathered, gathered, head.reshape(1, cols))
    return seg_kv, scores


def local(
    draft_tokens,
    draft_gate,
    draft_up,
    draft_head,
    verifier_rows,
    norm_gain,
    key_weight,
    value_weight,
    pool_query,
    flags,
    owner,
):
    seg_count = flags.shape[0]
    n_seq = lax.axis_size("seq")
    n_fsdp = lax.axis_size("fsdp")
    d_rows, d_cols = draft_gate.shape
    v_rows = key_weight.shape[0]
    kv_cols = key_weight.shape[1]
    kv_block = jnp.concatenate([key_weight, value_weight], axis=1)
    kv_block = kv_block.reshape(-1, d_cols)
    block = jnp.concatenate([kv_block, draft_gate, draft_up], axis=0)
    gathered = lax.all_gather(block, "fsdp", axis=0, tiled=False)
    kv_rows = kv_block.shape[0]

    normed = normalize_rows(verifier_rows, norm_gain)
    seg_kv, partial_scores = project_all(
        normed, draft_tokens, gathered, draft_head, kv_rows, d_rows, 4
    )
    seg_keys = seg_kv[:, :kv_cols]
    seg_values = seg_kv[:, kv_cols:]
    lane_pick = (
        owner[:, None] == jnp.arange(pool_query.shape[0], dtype=jnp.int32)[None, :]
    ).astype(jnp.float32)
    queries = jnp.einsum("sc,chd->shd", lane_pick, pool_query, precision=lax.Precision.HIGHEST)
    summary_key, summary_value = segment_pool(
        seg_keys.reshape(seg_count, SEGL, KVH, HD),
        seg_values.reshape(seg_count, SEGL, KVH, HD),
        queries,
        HD,
    )
    width = KVH * HD
    live_row = jnp.zeros((1, width), jnp.float32).at[0, :seg_count].set(flags.astype(jnp.float32))
    tail = jnp.concatenate(
        [
            partial_scores.reshape(-1, width),
            summary_key.reshape(seg_count, width),
            summary_value.reshape(seg_count, width),
            live_row,
        ],
        axis=0,
    )
    tail_all = jnp.stack(
        [tail]
        + [
            lax.ppermute(tail, "seq", [(i, (i + k) % n_seq) for i in range(n_seq)])
            for k in range(1, n_seq)
        ]
    )
    score_rows = partial_scores.size // width
    scores_all = tail_all[:, :score_rows].reshape(n_seq, -1)
    summary_all = tail_all[:, score_rows:]
    own = lax.axis_index("seq")
    own_tokens = seg_count * SEGL
    token_scores = jnp.sum(
        lax.dynamic_slice_in_dim(scores_all, own * own_tokens, own_tokens, axis=1), axis=0
    )
    draft_score = jnp.mean(token_scores.reshape(seg_count, SEGL), axis=1)
    key_all = summary_all[:, :seg_count].reshape(-1, KVH, HD)
    value_all = summary_all[:, seg_count : 2 * seg_count].reshape(-1, KVH, HD)
    live_all = summary_all[:, 2 * seg_count, :seg_count].reshape(-1)
    pooled = cross_pool(
        summary_key,
        key_all,
        value_all,
        live_all > 0.5,
        HD,
    )
    own_pooled = pooled.reshape(seg_count, KVH * HD)
    verdict = jnp.where(
        flags[:, None] == 1, jax.nn.sigmoid(draft_score)[:, None] * own_pooled, 0.0
    ).astype(jnp.bfloat16)
    return (draft_score, verdict)


def solution(mesh):
    return jax.shard_map(
        local,
        mesh=mesh,
        in_specs=(
            P("fsdp", None),
            P("fsdp", "seq"),
            P("fsdp", "seq"),
            P("seq"),
            P(("fsdp", "seq"), None),
            P(),
            P("fsdp", None),
            P("fsdp", None),
            P(),
            P(("fsdp", "seq")),
            P(("fsdp", "seq")),
        ),
        out_specs=(P(("fsdp", "seq")), P(("fsdp", "seq"), None)),
        check_vma=False,
    )
```
